512 devices in a mesh: seq: 16 (over y_lo, z), head: 8 (over x, core), dp: 4 (over y_hi).
Axes of the slice: x: 4, y: 8 (y_hi: 4, y_lo: 2; y = y_hi * 2 + y_lo), z: 8, core: 2. Of those that a mesh axis runs over, the one named last changes fastest.
Arguments:
- queries: bfloat16 [65536, 2048], P(('dp', 'seq', 'head')), parts along dimension 0, may hold values from -9 to 9
- keys: bfloat16 [65536, 2048], P(('dp', 'seq', 'head')), parts along dimension 0, may hold values from -9 to 9
- values: bfloat16 [65536, 2048], P(('dp', 'seq', 'head')), parts along dimension 0, may hold values from -6 to 6
- coords: int32 [3, 65536], P(None, ('dp', 'seq', 'head')), parts along dimension 1, may hold values from 0 to 511, as said below
- lengths: int32 [128], P('dp'), parts along dimension 0, may hold values from 1 to 1536, 16384 in all
Outputs:
- attention: bfloat16 [65536, 2048], P(('dp', 'seq', 'head')), parts along dimension 0
The draws below stay inside these ranges and needn't reach their ends.
There are 4 independent parts, one for each index of `dp`. The reference program is written for one: setup_inputs(seed, part) draws one part's arguments, and reference() takes and returns one part's arrays. A program takes and returns all parts, laid end to end along the dimension named above; each array names one. Nothing has to cross between parts.
Inputs may be any that keep to these rules, and one draw needn't show every extreme that they name: `coords`: voxel coordinates of each token along x, y and z. `lengths`: the token counts of the 32 scenes of a pack in order; they sum to 16384 and the longest scene has exactly 1536 tokens.
All inputs are finite; a program needn't handle non-finite values.
Results may differ from the reference program's by a relative error of at most 0.012.
Values may be sent and summed in bfloat16 or wider, within the bound.
No kernel may reach another device: no remote copies, remote signals or barrier semaphores. Data moves between devices by JAX's collectives and lax.ppermute only.
A program may use at most 128 MiB of HBM per device.

```python
import math
import jax
import jax.numpy as jnp
import numpy as np
from jax import lax

H = 32
HD = 64
SCENES = 32
GROUP = 1024
TOKENS = 16384
MOST = 1536
REACH = 2


def make_coords(key):
    return jax.random.randint(jax.random.fold_in(key, 11), (3, TOKENS), 0, 512).astype(jnp.int32)


def drawn_draw(key):
    return jnp.clip(jax.random.normal(key, (TOKENS, H * HD), jnp.float32), -6.0, 6.0)


def draw_coords(key, part):
    return make_coords(key)


def draw_queries(key, part):
    drawn = drawn_draw(jax.random.fold_in(key, 31))
    return drawn.astype(jnp.bfloat16)


def draw_keys(key, part):
    drawn = drawn_draw(jax.random.fold_in(key, 37))
    return drawn.astype(jnp.bfloat16)


def level_of(own_key, shape, shards, smallest, high):
    def one(dim, blocks):
        steps = jax.random.uniform(jax.random.fold_in(jax.random.fold_in(own_key, 6), dim), (blocks,), jnp.float32, smallest / len(shards), high / len(shards))
        return jnp.repeat(jnp.exp(steps), shape[dim] // blocks).reshape((-1,) + (1,) * (len(shape) - dim - 1))

    loudness = one(*shards[0])
    for cut in shards[1:]:
        loudness = loudness * one(*cut)
    return loudness


def length_profile(number_of, total, limit, slope):
    portions = [(1 << 20) // math.isqrt(rank ** slope) + 1 for rank in range(2, number_of + 1)]
    rest, counts = total - limit - (number_of - 1), [1] * (number_of - 1)
    while rest > 0:
        candidates = [i for i in range(number_of - 1) if counts[i] < limit]
        whole, left = sum([portions[i] for i in candidates]), rest
        for i in candidates:
            extra = min(limit - counts[i], max(1, left * portions[i] // whole), rest)
            counts[i] = counts[i] + extra
            rest = rest - extra
    return np.array([limit] + counts)


def ragged_sizes(rng, number_of, total, limit, lean):
    if number_of == 2:
        one = jax.random.randint(rng, (), max(1, total - limit), min(limit, total - 1) + 1)
        return jnp.stack([one, total - one])
    sizes = jnp.asarray(length_profile(number_of, total, limit, lean), jnp.int32)
    couples = (number_of - 1) // 2
    giver, sink = sizes[1:1 + 2 * couples:2], sizes[2:2 + 2 * couples:2]
    room = jnp.minimum(giver - 1, limit - sink)
    passed = jax.random.randint(jax.random.fold_in(rng, 1), (couples,), 0, 1 << 20) % (room + 1)
    sizes = sizes.at[1:1 + 2 * couples:2].set(giver - passed).at[2:2 + 2 * couples:2].set(sink + passed)
    return sizes[jax.random.permutation(jax.random.fold_in(rng, 2), number_of)]


def normal_values(rng, dims, deviation, limit, split=(), kind=jnp.bfloat16):
    values = deviation * jax.random.normal(rng, dims, jnp.float32)
    if split:
        values = values * level_of(rng, dims, split, -0.22, 0.18)
    return jnp.clip(values, -limit, limit).astype(kind)


def setup_inputs(seed: int = 0, part: int = 0) -> dict:
    key_list = jax.random.split(jax.random.key(seed), 6)
    part_splits = jax.random.split(jax.random.fold_in(key_list[5], part), 6)
    return {
        "queries": draw_queries(jax.random.fold_in(jax.random.fold_in(key_list[5], part), 71), part),
        "keys": draw_keys(jax.random.fold_in(jax.random.fold_in(key_list[5], part), 71), part),
        "values": normal_values(part_splits[2], (TOKENS, H * HD), 1.0, 6.0, ((0, 128),)),
        "coords": draw_coords(jax.random.fold_in(jax.random.fold_in(key_list[5], part), 71), part),
        "lengths": ragged_sizes(part_splits[4], SCENES, TOKENS, MOST, 2).astype(jnp.int32),
    }


score_scale = 0.125
neg_big = -1.0e30


def rotary_angles(coords):
    pair_count = HD // 2
    pair_id = jnp.arange(pair_count, dtype=jnp.int32)
    axis_of = (3 * pair_id) // pair_count
    exponent = ((3 * pair_id) % pair_count).astype(jnp.float32) / pair_count
    frequency = jnp.power(jnp.float32(100.0), -exponent)
    position = coords.astype(jnp.float32)
    angles = jnp.zeros((coords.shape[1], pair_count), jnp.float32)
    for axis_id in range(3):
        picked = jnp.where(axis_of == axis_id, frequency, jnp.float32(0.0))
        angles = angles + position[axis_id][:, None] * picked[None, :]
    return angles


def rotate_rows(source, angles):
    row_count = source.shape[0]
    per_head = source.reshape(row_count, -1, HD).astype(jnp.float32)
    half_size = HD // 2
    front_half = per_head[..., :half_size]
    back_half = per_head[..., half_size:]
    cos_val = jnp.cos(angles)[:, None, :]
    sin_val = jnp.sin(angles)[:, None, :]
    turned = jnp.concatenate([front_half * cos_val - back_half * sin_val, front_half * sin_val + back_half * cos_val], axis=-1)
    return turned.reshape(row_count, -1)


def scene_of(positions, lengths):
    scene_end = jnp.cumsum(lengths).astype(jnp.int32)
    return jnp.sum((positions[:, None] >= scene_end[None, :]).astype(jnp.int32), axis=1).astype(jnp.int32)


def reference(queries, keys, values, coords, lengths):
    angles = rotary_angles(coords)
    q_heads = rotate_rows(queries, angles).astype(jnp.bfloat16).reshape(TOKENS, H, HD).transpose(1, 0, 2)
    k_heads = rotate_rows(keys, angles).astype(jnp.bfloat16).reshape(TOKENS, H, HD).transpose(1, 0, 2)
    v_heads = values.reshape(TOKENS, H, HD).transpose(1, 0, 2)
    scene = scene_of(jnp.arange(TOKENS, dtype=jnp.int32), lengths)
    margin = REACH * GROUP
    window = (2 * REACH + 1) * GROUP
    scene_pad = jnp.pad(scene, (margin, margin), constant_values=-1).astype(jnp.int32)
    block_starts = (jnp.arange(TOKENS // GROUP, dtype=jnp.int32) * GROUP).astype(jnp.int32)

    def one_head(operands):
        q_one, k_one, v_one = operands
        k_pad = jnp.pad(k_one, ((margin, margin), (0, 0)))
        v_pad = jnp.pad(v_one, ((margin, margin), (0, 0)))

        def one_block(block_start):
            query_block = lax.dynamic_slice_in_dim(q_one, block_start, GROUP, 0)
            query_scene = lax.dynamic_slice_in_dim(scene, block_start, GROUP, 0)
            key_block = lax.dynamic_slice_in_dim(k_pad, block_start, window, 0)
            value_block = lax.dynamic_slice_in_dim(v_pad, block_start, window, 0)
            key_scene = lax.dynamic_slice_in_dim(scene_pad, block_start, window, 0)
            scores = jnp.dot(query_block, key_block.T, preferred_element_type=jnp.float32) * score_scale
            allowed = query_scene[:, None] == key_scene[None, :]
            row_top = jnp.max(jnp.where(allowed, scores, neg_big), axis=1, keepdims=True)
            raw_weights = jnp.where(allowed, jnp.exp(scores - row_top), jnp.float32(0.0))
            weight_sum = jnp.sum(raw_weights, axis=1, keepdims=True)
            mixed = jnp.dot(raw_weights.astype(jnp.bfloat16), value_block, preferred_element_type=jnp.float32)
            return mixed / weight_sum

        return lax.map(one_block, block_starts).reshape(TOKENS, HD)

    result = lax.map(one_head, (q_heads, k_heads, v_heads))
    return result.transpose(1, 0, 2).reshape(TOKENS, H * HD).astype(jnp.bfloat16)
```

```python
import functools

import jax
import jax.numpy as jnp
from jax import lax
from jax.experimental import pallas as pl
from jax.experimental.pallas import tpu as pltpu
from jax.sharding import PartitionSpec as P

HD = 64
MOST = 1536

score_scale = 0.125
neg_big = -1e30

TQ = 256
TK = 512


def shifted(block, axis, distance):
    devices = range(lax.axis_size(axis))
    route = [(i - distance, i) for i in devices if i - distance in devices]
    return lax.ppermute(block, axis, route)


def rotary_angles(coords):
    pair_count = HD // 2
    pair_id = jnp.arange(pair_count, dtype=jnp.int32)
    axis_of = 3 * pair_id // pair_count
    exponent = (3 * pair_id % pair_count).astype(jnp.float32) / pair_count
    frequency = jnp.power(jnp.float32(100.0), -exponent)
    position = coords.astype(jnp.float32)
    angles = jnp.zeros((coords.shape[1], pair_count), jnp.float32)
    for axis_id in range(3):
        picked = jnp.where(axis_of == axis_id, frequency, jnp.float32(0.0))
        angles = angles + position[axis_id][:, None] * picked[None, :]
    return angles


def rotate_rows(source, angles):
    row_count = source.shape[0]
    per_head = source.reshape(row_count, -1, HD).astype(jnp.float32)
    half_size = HD // 2
    front_half = per_head[..., :half_size]
    back_half = per_head[..., half_size:]
    cos_val = jnp.cos(angles)[:, None, :]
    sin_val = jnp.sin(angles)[:, None, :]
    turned = jnp.concatenate(
        [front_half * cos_val - back_half * sin_val, front_half * sin_val + back_half * cos_val],
        axis=-1,
    )
    return turned.reshape(row_count, -1)


def scene_of(positions, scene_end):
    return jnp.sum((positions[:, None] >= scene_end[None, :]).astype(jnp.int32), axis=1)


def flash_kernel(klo_ref, khi_ref, q_ref, k_ref, v_ref, qs_ref, ks_ref, o_ref):
    i = pl.program_id(1)
    q = q_ref[0]
    qs = qs_ref[...]
    tq = q.shape[0]

    def body(j, carry):
        m, l, acc = carry
        start = pl.multiple_of(j * TK, TK)
        k = k_ref[0, 0, pl.ds(start, TK), :]
        v = v_ref[0, 0, pl.ds(start, TK), :]
        ks = ks_ref[:, pl.ds(start, TK)]
        s = lax.dot_general(
            q, k, (((1,), (1,)), ((), ())), preferred_element_type=jnp.float32
        ) * score_scale
        s = jnp.where(qs == ks, s, neg_big)
        m_new = jnp.maximum(m, jnp.max(s, axis=1, keepdims=True))
        p = jnp.exp(s - m_new)
        alpha = jnp.exp(m - m_new)
        l = l * alpha + jnp.sum(p, axis=1, keepdims=True)
        acc = acc * alpha + jnp.dot(
            p.astype(jnp.bfloat16), v, preferred_element_type=jnp.float32
        )
        return m_new, l, acc

    init = (
        jnp.full((tq, 1), neg_big, jnp.float32),
        jnp.zeros((tq, 1), jnp.float32),
        jnp.zeros((tq, HD), jnp.float32),
    )
    m, l, acc = lax.fori_loop(klo_ref[i], khi_ref[i], body, init)
    o_ref[0] = (acc / l).astype(o_ref.dtype)


def flash(klo, khi, q_h, kv_win, q_scene, k_scene):
    heads, qlen, _ = q_h.shape
    wlen = kv_win.shape[2]
    grid = (heads, qlen // TQ)
    return pl.pallas_call(
        flash_kernel,
        out_shape=jax.ShapeDtypeStruct((heads, qlen, HD), jnp.bfloat16),
        grid_spec=pltpu.PrefetchScalarGridSpec(
            num_scalar_prefetch=2,
            grid=grid,
            in_specs=[
                pl.BlockSpec((1, TQ, HD), lambda h, i, *_: (h, i, 0)),
                pl.BlockSpec((1, 1, wlen, HD), lambda h, i, *_: (0, h, 0, 0)),
                pl.BlockSpec((1, 1, wlen, HD), lambda h, i, *_: (1, h, 0, 0)),
                pl.BlockSpec((TQ, 1), lambda h, i, *_: (i, 0)),
                pl.BlockSpec((1, wlen), lambda h, i, *_: (0, 0)),
            ],
            out_specs=pl.BlockSpec((1, TQ, HD), lambda h, i, *_: (h, i, 0)),
        ),
        compiler_params=pltpu.CompilerParams(
            dimension_semantics=("arbitrary", "arbitrary")
        ),
    )(klo, khi, q_h, kv_win, kv_win, q_scene, k_scene)


def local(queries, keys, values, coords, lengths):
    tok_dev, all_cols = queries.shape
    head_count = lax.axis_size("head")
    seq_count = lax.axis_size("seq")
    head_cols = all_cols // head_count
    local_heads = head_cols // HD
    group_len = tok_dev * head_count
    total_len = group_len * seq_count
    near = min(MOST, group_len)
    far = MOST - near
    angles = rotary_angles(coords)
    q_rot = rotate_rows(queries, angles).astype(jnp.bfloat16)
    k_rot = rotate_rows(keys, angles).astype(jnp.bfloat16)
    qkv = jnp.stack([q_rot, k_rot, values]).reshape(3, tok_dev, head_count, head_cols)
    blk = lax.all_to_all(qkv, "head", split_axis=2, concat_axis=1, tiled=True)
    blk = blk.reshape(3, group_len, local_heads, HD).transpose(0, 2, 1, 3)
    q_h = blk[0]
    kv = blk[1:]
    pieces = [kv]
    below = [shifted(kv, "seq", 1)]
    above = [shifted(kv, "seq", -1)]
    if far > 0:
        below.insert(0, shifted(kv[:, :, group_len - far:], "seq", 2))
        above.append(shifted(kv[:, :, :far], "seq", -2))
    kv_win = jnp.concatenate(below + pieces + above, axis=2)
    own_start = lax.axis_index("seq") * group_len
    win_start = own_start - group_len - far
    wlen = kv_win.shape[2]

    scene_end = jnp.cumsum(lengths).astype(jnp.int32)
    scene_begin = scene_end - lengths
    q_pos = own_start + jnp.arange(group_len, dtype=jnp.int32)
    q_scene = scene_of(q_pos, scene_end)
    k_pos = win_start + jnp.arange(wlen, dtype=jnp.int32)
    k_valid = (k_pos >= 0) & (k_pos < total_len)
    k_scene = jnp.where(k_valid, scene_of(k_pos, scene_end), -1)

    first_scene = q_scene[::TQ]
    last_scene = q_scene[TQ - 1 :: TQ]
    lo = jnp.take(scene_begin, first_scene) - win_start
    hi = jnp.take(scene_end, last_scene) - win_start
    lo = jnp.clip(lo, 0, wlen)
    hi = jnp.clip(hi, 0, wlen)
    klo = (lo // TK).astype(jnp.int32)
    khi = ((hi + TK - 1) // TK).astype(jnp.int32)

    out_h = flash(
        klo,
        khi,
        q_h,
        kv_win,
        q_scene.reshape(group_len, 1),
        k_scene.reshape(1, wlen).astype(jnp.int32),
    )
    finished = out_h.transpose(1, 0, 2).reshape(group_len, head_cols)
    returned = lax.all_to_all(
        finished.reshape(group_len, 1, head_cols), "head", split_axis=0, concat_axis=1, tiled=True
    )
    return returned.reshape(tok_dev, all_cols)


def solution(mesh):
    in_specs = (
        P(("dp", "seq", "head"), None),
        P(("dp", "seq", "head"), None),
        P(("dp", "seq", "head"), None),
        P(None, ("dp", "seq", "head")),
        P("dp"),
    )
    out_specs = P(("dp", "seq", "head"), None)
    return jax.shard_map(local, mesh=mesh, in_specs=in_specs, out_specs=out_specs, check_vma=False)
```

```python
import jax
import jax.numpy as jnp
from jax import lax
from jax.experimental import pallas as pl
from jax.experimental.pallas import tpu as pltpu
from jax.sharding import PartitionSpec as P

HD = 64
MOST = 1536

score_scale = 0.125
neg_big = -1e30

TQ = 256
TK = 256


def shifted(block, axis, distance):
    devices = range(lax.axis_size(axis))
    route = [(i - distance, i) for i in devices if i - distance in devices]
    return lax.ppermute(block, axis, route)


def rotary_angles(coords):
    pair_count = HD // 2
    pair_id = jnp.arange(pair_count, dtype=jnp.int32)
    axis_of = 3 * pair_id // pair_count
    exponent = (3 * pair_id % pair_count).astype(jnp.float32) / pair_count
    frequency = jnp.power(jnp.float32(100.0), -exponent)
    position = coords.astype(jnp.float32)
    angles = jnp.zeros((coords.shape[1], pair_count), jnp.float32)
    for axis_id in range(3):
        picked = jnp.where(axis_of == axis_id, frequency, jnp.float32(0.0))
        angles = angles + position[axis_id][:, None] * picked[None, :]
    return angles


def rotate_rows(source, angles, scale=None):
    row_count = source.shape[0]
    per_head = source.reshape(row_count, -1, HD).astype(jnp.float32)
    half_size = HD // 2
    front_half = per_head[..., :half_size]
    back_half = per_head[..., half_size:]
    cos_val = jnp.cos(angles)[:, None, :]
    sin_val = jnp.sin(angles)[:, None, :]
    turned = jnp.concatenate(
        [front_half * cos_val - back_half * sin_val, front_half * sin_val + back_half * cos_val],
        axis=-1,
    )
    if scale is not None:
        turned = turned * jnp.float32(scale)
    return turned


def scene_of(positions, scene_end):
    return jnp.sum((positions[:, None] >= scene_end[None, :]).astype(jnp.int32), axis=1)


def make_kernel(piece_rows, nq, has_state, finalize):
    n_pieces = len(piece_rows)
    ktmax = max(piece_rows) // TK

    def kernel(lo_ref, hi_ref, full_ref, q_ref, qs_ref, *rest):
        piece_refs = rest[: 3 * n_pieces]
        rest = rest[3 * n_pieces :]
        if has_state:
            m_in, l_in, acc_in = rest[:3]
            rest = rest[3:]
        outs = rest
        i = pl.program_id(1)
        q = q_ref[0, 0]
        qs = qs_ref[...]
        tq = q.shape[0]
        if has_state:
            carry = (m_in[0], l_in[0], acc_in[0])
        else:
            carry = (
                jnp.full((tq, 1), neg_big, jnp.float32),
                jnp.zeros((tq, 1), jnp.float32),
                jnp.zeros((tq, HD), jnp.float32),
            )
        for p in range(n_pieces):
            k_ref, v_ref, ks_ref = piece_refs[3 * p : 3 * p + 3]
            base = p * nq + i

            def update(start, carry, masked, k_ref=k_ref, v_ref=v_ref, ks_ref=ks_ref):
                m, l, acc = carry
                k = k_ref[0, 0, pl.ds(start, TK), :]
                v = v_ref[0, 0, pl.ds(start, TK), :]
                s = lax.dot_general(
                    q, k, (((1,), (1,)), ((), ())), preferred_element_type=jnp.float32
                )
                if masked:
                    ks = ks_ref[:, pl.ds(start, TK)]
                    s = jnp.where(qs == ks, s, neg_big)
                m_new = jnp.maximum(m, jnp.max(s, axis=1, keepdims=True))
                p_w = jnp.exp(s - m_new)
                alpha = jnp.exp(m - m_new)
                l = l * alpha + jnp.sum(p_w, axis=1, keepdims=True)
                acc = acc * alpha + jnp.dot(
                    p_w.astype(jnp.bfloat16), v, preferred_element_type=jnp.float32
                )
                return m_new, l, acc

            def body(j, carry, base=base, update=update):
                start = pl.multiple_of(j * TK, TK)
                full = full_ref[base * ktmax + j]
                return lax.cond(
                    full != 0,
                    lambda c: update(start, c, False),
                    lambda c: update(start, c, True),
                    carry,
                )

            carry = lax.fori_loop(lo_ref[base], hi_ref[base], body, carry)
        m, l, acc = carry
        if finalize:
            outs[0][0, 0] = (acc / l).astype(outs[0].dtype)
        else:
            outs[0][0] = m
            outs[1][0] = l
            outs[2][0] = acc

    return kernel


def attend(q_h, q_scene, pieces, lo, hi, full, state):
    heads, qlen, _ = q_h.shape[1:] if q_h.ndim == 4 else q_h.shape
    nq = qlen // TQ
    piece_rows = [kv.shape[2] for kv, _ in pieces]
    has_state = state is not None
    finalize = has_state
    kernel = make_kernel(piece_rows, nq, has_state, finalize)
    in_specs = [
        pl.BlockSpec((1, 1, TQ, HD), lambda h, i, *_: (0, h, i, 0)),
        pl.BlockSpec((TQ, 1), lambda h, i, *_: (i, 0)),
    ]
    args = [q_h, q_scene]
    for kv, ks in pieces:
        rows = kv.shape[2]
        in_specs.append(pl.BlockSpec((1, 1, rows, HD), lambda h, i, *_: (0, h, 0, 0)))
        in_specs.append(pl.BlockSpec((1, 1, rows, HD), lambda h, i, *_: (1, h, 0, 0)))
        in_specs.append(pl.BlockSpec((1, rows), lambda h, i, *_: (0, 0)))
        args += [kv, kv, ks]
    state_specs = [
        pl.BlockSpec((1, TQ, 1), lambda h, i, *_: (h, i, 0)),
        pl.BlockSpec((1, TQ, 1), lambda h, i, *_: (h, i, 0)),
        pl.BlockSpec((1, TQ, HD), lambda h, i, *_: (h, i, 0)),
    ]
    state_shapes = [
        jax.ShapeDtypeStruct((heads, qlen, 1), jnp.float32),
        jax.ShapeDtypeStruct((heads, qlen, 1), jnp.float32),
        jax.ShapeDtypeStruct((heads, qlen, HD), jnp.float32),
    ]
    if has_state:
        in_specs += state_specs
        args += list(state)
    if finalize:
        out_specs = [pl.BlockSpec((1, 1, TQ, HD), lambda h, i, *_: (0, h, i, 0))]
        out_shape = [jax.ShapeDtypeStruct((1, heads, qlen, HD), jnp.bfloat16)]
    else:
        out_specs = state_specs
        out_shape = state_shapes
    return pl.pallas_call(
        kernel,
        out_shape=out_shape,
        grid_spec=pltpu.PrefetchScalarGridSpec(
            num_scalar_prefetch=3,
            grid=(heads, nq),
            in_specs=in_specs,
            out_specs=out_specs,
        ),
        compiler_params=pltpu.CompilerParams(
            dimension_semantics=("arbitrary", "arbitrary")
        ),
    )(lo, hi, full, *args)


def local(queries, keys, values, coords, lengths):
    tok_dev, all_cols = queries.shape
    head_count = lax.axis_size("head")
    seq_count = lax.axis_size("seq")
    head_cols = all_cols // head_count
    local_heads = head_cols // HD
    group_len = tok_dev * head_count
    total_len = group_len * seq_count
    near = min(MOST, group_len)
    far = MOST - near
    nq = group_len // TQ

    def head_major(x):
        return x.reshape(tok_dev, head_count, local_heads, HD).transpose(1, 2, 0, 3)

    angles = rotary_angles(coords)
    q_rot = head_major(rotate_rows(queries, angles, score_scale).astype(jnp.bfloat16))
    k_rot = head_major(rotate_rows(keys, angles).astype(jnp.bfloat16))
    v_hm = head_major(values)
    kv_src = jnp.stack([k_rot, v_hm])
    kv = lax.all_to_all(kv_src, "head", split_axis=1, concat_axis=3, tiled=True)
    kv = kv.reshape(2, local_heads, group_len, HD)
    q_h = lax.all_to_all(q_rot, "head", split_axis=0, concat_axis=2, tiled=True)

    below1 = shifted(kv, "seq", 1)
    above1 = shifted(kv, "seq", -1)
    halo = [(below1, -group_len), (above1, group_len)]
    if far > 0:
        below2 = shifted(kv[:, :, group_len - far :], "seq", 2)
        above2 = shifted(kv[:, :, :far], "seq", -2)
        halo = [(below2, -group_len - far)] + halo + [(above2, 2 * group_len)]

    own_start = lax.axis_index("seq") * group_len
    scene_end = jnp.cumsum(lengths).astype(jnp.int32)
    scene_begin = scene_end - lengths
    q_pos = own_start + jnp.arange(group_len, dtype=jnp.int32)
    q_scene = scene_of(q_pos, scene_end)
    first_scene = q_scene[::TQ]
    last_scene = q_scene[TQ - 1 :: TQ]
    span_lo = jnp.take(scene_begin, first_scene)
    span_hi = jnp.take(scene_end, last_scene)
    q_single = first_scene == last_scene

    def tables(piece_list):
        ktmax = max(kvp.shape[2] for kvp, _ in piece_list) // TK
        los, his, fulls, prepared = [], [], [], []
        for kvp, offset in piece_list:
            rows = kvp.shape[2]
            p0 = own_start + offset
            k_pos = p0 + jnp.arange(rows, dtype=jnp.int32)
            k_valid = (k_pos >= 0) & (k_pos < total_len)
            k_scene = jnp.where(k_valid, scene_of(k_pos, scene_end), -1).astype(jnp.int32)
            lo = jnp.clip(span_lo - p0, 0, rows)
            hi = jnp.clip(span_hi - p0, 0, rows)
            klo = lo // TK
            khi = jnp.maximum((hi + TK - 1) // TK, klo)
            los.append(klo)
            his.append(khi)
            kt_first = k_scene[::TK]
            kt_last = k_scene[TK - 1 :: TK]
            kfull = (
                q_single[:, None]
                & (kt_first[None, :] == first_scene[:, None])
                & (kt_last[None, :] == first_scene[:, None])
            )
            kfull = jnp.pad(kfull, ((0, 0), (0, ktmax - kfull.shape[1])))
            fulls.append(kfull.reshape(-1))
            prepared.append((kvp, k_scene.reshape(1, rows)))
        return (
            jnp.concatenate(los).astype(jnp.int32),
            jnp.concatenate(his).astype(jnp.int32),
            jnp.concatenate(fulls).astype(jnp.int32),
            prepared,
        )

    q_scene_col = q_scene.reshape(group_len, 1).astype(jnp.int32)
    lo0, hi0, full0, prep0 = tables([(kv, 0)])
    state = attend(q_h, q_scene_col, prep0, lo0, hi0, full0, None)
    lo1, hi1, full1, prep1 = tables(halo)
    out_h = attend(q_h, q_scene_col, prep1, lo1, hi1, full1, state)[0]

    out_src = out_h.reshape(local_heads, head_count, tok_dev, HD)
    back = lax.all_to_all(out_src, "head", split_axis=1, concat_axis=0, tiled=True)
    back = back.reshape(head_count * local_heads, tok_dev, HD)
    return back.transpose(1, 0, 2).reshape(tok_dev, all_cols)


def solution(mesh):
    in_specs = (
        P(("dp", "seq", "head"), None),
        P(("dp", "seq", "head"), None),
        P(("dp", "seq", "head"), None),
        P(None, ("dp", "seq", "head")),
        P("dp"),
    )
    out_specs = P(("dp", "seq", "head"), None)
    return jax.shard_map(local, mesh=mesh, in_specs=in_specs, out_specs=out_specs, check_vma=False)
```

```python
import jax
import jax.numpy as jnp
from jax import lax
from jax.experimental import pallas as pl
from jax.experimental.pallas import tpu as pltpu
from jax.sharding import PartitionSpec as P

HD = 64
MOST = 1536

score_scale = 0.125
neg_big = -1e30

TQ = 256
TK = 256


def shifted(block, axis, distance):
    devices = range(lax.axis_size(axis))
    route = [(i - distance, i) for i in devices if i - distance in devices]
    return lax.ppermute(block, axis, route)


def rotary_angles(coords):
    pair_count = HD // 2
    pair_id = jnp.arange(pair_count, dtype=jnp.int32)
    axis_of = 3 * pair_id // pair_count
    exponent = (3 * pair_id % pair_count).astype(jnp.float32) / pair_count
    frequency = jnp.power(jnp.float32(100.0), -exponent)
    position = coords.astype(jnp.float32)
    angles = jnp.zeros((coords.shape[1], pair_count), jnp.float32)
    for axis_id in range(3):
        picked = jnp.where(axis_of == axis_id, frequency, jnp.float32(0.0))
        angles = angles + position[axis_id][:, None] * picked[None, :]
    return angles


def rotate_rows(source, angles, scale=None):
    row_count = source.shape[0]
    per_head = source.reshape(row_count, -1, HD).astype(jnp.float32)
    half_size = HD // 2
    front_half = per_head[..., :half_size]
    back_half = per_head[..., half_size:]
    cos_val = jnp.cos(angles)[:, None, :]
    sin_val = jnp.sin(angles)[:, None, :]
    turned = jnp.concatenate(
        [front_half * cos_val - back_half * sin_val, front_half * sin_val + back_half * cos_val],
        axis=-1,
    )
    if scale is not None:
        turned = turned * jnp.float32(scale)
    return turned


def scene_of(positions, scene_end):
    return jnp.sum((positions[:, None] >= scene_end[None, :]).astype(jnp.int32), axis=1)


LANES = 128


def make_kernel(piece_rows, nq, has_state, finalize):
    n_pieces = len(piece_rows)

    def kernel(lo_ref, hi_ref, q_ref, qs_ref, *rest):
        piece_refs = rest[: 2 * n_pieces]
        rest = rest[2 * n_pieces :]
        if has_state:
            m_in, l_in, acc_in = rest[:3]
            rest = rest[3:]
        outs = rest
        i = pl.program_id(1)
        q = q_ref[0, 0]
        qs = jnp.tile(qs_ref[...], (1, TK // LANES))
        tq = q.shape[0]
        if has_state:
            carry = (m_in[0], l_in[0], acc_in[0])
        else:
            carry = (
                jnp.full((tq, LANES), neg_big, jnp.float32),
                jnp.zeros((tq, LANES), jnp.float32),
                jnp.zeros((tq, HD), jnp.float32),
            )
        for p in range(n_pieces):
            kv_ref, ks_ref = piece_refs[2 * p : 2 * p + 2]
            base = p * nq + i

            def body(j, carry, kv_ref=kv_ref, ks_ref=ks_ref):
                m, l, acc = carry
                start = pl.multiple_of(j * TK, TK)
                k = kv_ref[0, 0, pl.ds(start, TK), :]
                v = kv_ref[1, 0, pl.ds(start, TK), :]
                ks = ks_ref[:, pl.ds(start, TK)]
                s = lax.dot_general(
                    q, k, (((1,), (1,)), ((), ())), preferred_element_type=jnp.float32
                )
                s = jnp.where(qs == ks, s, neg_big)
                m_new = jnp.maximum(m, jnp.max(s, axis=1)[:, None])
                p_w = jnp.exp(s - jnp.tile(m_new, (1, TK // LANES)))
                alpha = jnp.exp(m - m_new)
                l = alpha * l + jnp.sum(p_w, axis=1)[:, None]
                acc = acc * alpha[:, :HD] + jnp.dot(
                    p_w.astype(jnp.bfloat16), v, preferred_element_type=jnp.float32
                )
                return m_new, l, acc

            carry = lax.fori_loop(lo_ref[base], hi_ref[base], body, carry)
        m, l, acc = carry
        if finalize:
            outs[0][0, 0] = (acc / l[:, :HD]).astype(outs[0].dtype)
        else:
            outs[0][0] = m
            outs[1][0] = l
            outs[2][0] = acc

    return kernel


def attend(q_h, q_scene, pieces, lo, hi, state):
    heads, qlen, _ = q_h.shape[1:]
    nq = qlen // TQ
    piece_rows = [kv.shape[2] for kv, _ in pieces]
    has_state = state is not None
    finalize = has_state
    kernel = make_kernel(piece_rows, nq, has_state, finalize)
    in_specs = [
        pl.BlockSpec((1, 1, TQ, HD), lambda h, i, *_: (0, h, i, 0)),
        pl.BlockSpec((TQ, LANES), lambda h, i, *_: (i, 0)),
    ]
    args = [q_h, q_scene]
    for kv, ks in pieces:
        rows = kv.shape[2]
        in_specs.append(pl.BlockSpec((2, 1, rows, HD), lambda h, i, *_: (0, h, 0, 0)))
        in_specs.append(pl.BlockSpec((1, rows), lambda h, i, *_: (0, 0)))
        args += [kv, ks]
    state_specs = [
        pl.BlockSpec((1, TQ, LANES), lambda h, i, *_: (h, i, 0)),
        pl.BlockSpec((1, TQ, LANES), lambda h, i, *_: (h, i, 0)),
        pl.BlockSpec((1, TQ, HD), lambda h, i, *_: (h, i, 0)),
    ]
    state_shapes = [
        jax.ShapeDtypeStruct((heads, qlen, LANES), jnp.float32),
        jax.ShapeDtypeStruct((heads, qlen, LANES), jnp.float32),
        jax.ShapeDtypeStruct((heads, qlen, HD), jnp.float32),
    ]
    if has_state:
        in_specs += state_specs
        args += list(state)
    if finalize:
        out_specs = [pl.BlockSpec((1, 1, TQ, HD), lambda h, i, *_: (0, h, i, 0))]
        out_shape = [jax.ShapeDtypeStruct((1, heads, qlen, HD), jnp.bfloat16)]
    else:
        out_specs = state_specs
        out_shape = state_shapes
    return pl.pallas_call(
        kernel,
        out_shape=out_shape,
        grid_spec=pltpu.PrefetchScalarGridSpec(
            num_scalar_prefetch=2,
            grid=(heads, nq),
            in_specs=in_specs,
            out_specs=out_specs,
        ),
        compiler_params=pltpu.CompilerParams(
            dimension_semantics=("arbitrary", "arbitrary")
        ),
    )(lo, hi, *args)


def local(queries, keys, values, coords, lengths):
    tok_dev, all_cols = queries.shape
    head_count = lax.axis_size("head")
    seq_count = lax.axis_size("seq")
    head_cols = all_cols // head_count
    local_heads = head_cols // HD
    group_len = tok_dev * head_count
    total_len = group_len * seq_count
    near = min(MOST, group_len)
    far = MOST - near
    nq = group_len // TQ

    def head_major(x):
        return x.reshape(tok_dev, head_count, local_heads, HD).transpose(1, 2, 0, 3)

    angles = rotary_angles(coords)
    q_rot = head_major(rotate_rows(queries, angles, score_scale).astype(jnp.bfloat16))
    k_rot = head_major(rotate_rows(keys, angles).astype(jnp.bfloat16))
    v_hm = head_major(values)
    kv_src = jnp.stack([k_rot, v_hm])
    kv = lax.all_to_all(kv_src, "head", split_axis=1, concat_axis=3, tiled=True)
    kv = kv.reshape(2, local_heads, group_len, HD)
    q_h = lax.all_to_all(q_rot, "head", split_axis=0, concat_axis=2, tiled=True)

    below1 = shifted(kv, "seq", 1)
    above1 = shifted(kv, "seq", -1)
    halo = [(below1, -group_len), (above1, group_len)]
    if far > 0:
        below2 = shifted(kv[:, :, group_len - far :], "seq", 2)
        above2 = shifted(kv[:, :, :far], "seq", -2)
        halo = [(below2, -group_len - far)] + halo + [(above2, 2 * group_len)]

    own_start = lax.axis_index("seq") * group_len
    scene_end = jnp.cumsum(lengths).astype(jnp.int32)
    scene_begin = scene_end - lengths
    q_pos = own_start + jnp.arange(group_len, dtype=jnp.int32)
    q_scene = scene_of(q_pos, scene_end)
    first_scene = q_scene[::TQ]
    last_scene = q_scene[TQ - 1 :: TQ]
    span_lo = jnp.take(scene_begin, first_scene)
    span_hi = jnp.take(scene_end, last_scene)

    def tables(piece_list):
        los, his, prepared = [], [], []
        for kvp, offset in piece_list:
            rows = kvp.shape[2]
            p0 = own_start + offset
            k_pos = p0 + jnp.arange(rows, dtype=jnp.int32)
            k_valid = (k_pos >= 0) & (k_pos < total_len)
            k_scene = jnp.where(k_valid, scene_of(k_pos, scene_end), -1).astype(jnp.int32)
            lo = jnp.clip(span_lo - p0, 0, rows)
            hi = jnp.clip(span_hi - p0, 0, rows)
            klo = lo // TK
            khi = jnp.maximum((hi + TK - 1) // TK, klo)
            los.append(klo)
            his.append(khi)
            prepared.append((kvp, k_scene.reshape(1, rows)))
        return (
            jnp.concatenate(los).astype(jnp.int32),
            jnp.concatenate(his).astype(jnp.int32),
            prepared,
        )

    q_scene_col = jnp.broadcast_to(q_scene.astype(jnp.int32)[:, None], (group_len, LANES))
    lo0, hi0, prep0 = tables([(kv, 0)])
    state = attend(q_h, q_scene_col, prep0, lo0, hi0, None)
    lo1, hi1, prep1 = tables(halo)
    out_h = attend(q_h, q_scene_col, prep1, lo1, hi1, state)[0]

    out_src = out_h.reshape(local_heads, head_count, tok_dev, HD)
    back = lax.all_to_all(out_src, "head", split_axis=1, concat_axis=0, tiled=True)
    back = back.reshape(head_count * local_heads, tok_dev, HD)
    return back.transpose(1, 0, 2).reshape(tok_dev, all_cols)


def solution(mesh):
    in_specs = (
        P(("dp", "seq", "head"), None),
        P(("dp", "seq", "head"), None),
        P(("dp", "seq", "head"), None),
        P(None, ("dp", "seq", "head")),
        P("dp"),
    )
    out_specs = P(("dp", "seq", "head"), None)
    return jax.shard_map(local, mesh=mesh, in_specs=in_specs, out_specs=out_specs, check_vma=False)
```

```python
import jax
import jax.numpy as jnp
from jax import lax
from jax.experimental import pallas as pl
from jax.experimental.pallas import tpu as pltpu
from jax.sharding import PartitionSpec as P

HD = 64
MOST = 1536

score_scale = 0.125
neg_big = -1e30

TQ = 256
TK = 512


def shifted(block, axis, distance):
    devices = range(lax.axis_size(axis))
    route = [(i - distance, i) for i in devices if i - distance in devices]
    return lax.ppermute(block, axis, route)


def rotary_angles(coords):
    pair_count = HD // 2
    pair_id = jnp.arange(pair_count, dtype=jnp.int32)
    axis_of = 3 * pair_id // pair_count
    exponent = (3 * pair_id % pair_count).astype(jnp.float32) / pair_count
    frequency = jnp.power(jnp.float32(100.0), -exponent)
    position = coords.astype(jnp.float32)
    angles = jnp.zeros((coords.shape[1], pair_count), jnp.float32)
    for axis_id in range(3):
        picked = jnp.where(axis_of == axis_id, frequency, jnp.float32(0.0))
        angles = angles + position[axis_id][:, None] * picked[None, :]
    return angles


def rotate_rows(source, angles, scale=None):
    row_count = source.shape[0]
    per_head = source.reshape(row_count, -1, HD).astype(jnp.float32)
    half_size = HD // 2
    front_half = per_head[..., :half_size]
    back_half = per_head[..., half_size:]
    cos_val = jnp.cos(angles)[:, None, :]
    sin_val = jnp.sin(angles)[:, None, :]
    turned = jnp.concatenate(
        [front_half * cos_val - back_half * sin_val, front_half * sin_val + back_half * cos_val],
        axis=-1,
    )
    if scale is not None:
        turned = turned * jnp.float32(scale)
    return turned


def scene_of(positions, scene_end):
    return jnp.sum((positions[:, None] >= scene_end[None, :]).astype(jnp.int32), axis=1)


LANES = 128


def make_kernel(piece_rows, heads, nq, has_state, finalize):
    n_pieces = len(piece_rows)

    def kernel(lo_ref, hi_ref, q_ref, qs_ref, *rest):
        piece_refs = rest[: 2 * n_pieces]
        rest = rest[2 * n_pieces :]
        if has_state:
            m_in, acc_in = rest[:2]
            rest = rest[2:]
        outs = rest
        i = pl.program_id(0)
        tq = q_ref.shape[1]
        pad = jnp.zeros((tq, LANES - HD), jnp.bfloat16)
        qx = [jnp.concatenate([q_ref[h], pad], axis=1) for h in range(heads)]
        qs = jnp.tile(qs_ref[...], (1, TK // LANES))
        ones = jnp.ones((TK, LANES), jnp.bfloat16)
        two = 2 * LANES
        if has_state:
            carry = tuple((m_in[h], acc_in[h]) for h in range(heads))
        else:
            carry = tuple(
                (
                    jnp.full((tq, LANES), neg_big, jnp.float32),
                    jnp.zeros((tq, two), jnp.float32),
                )
                for h in range(heads)
            )
        for p in range(n_pieces):
            kv_ref, ks_ref = piece_refs[2 * p : 2 * p + 2]
            base = p * nq + i

            def body(j, carry, kv_ref=kv_ref, ks_ref=ks_ref):
                start = pl.multiple_of(j * TK, TK)
                allowed = qs == ks_ref[:, pl.ds(start, TK)]
                new = []
                for h in range(heads):
                    m, acc = carry[h]
                    kvt = kv_ref[h, pl.ds(start, TK), :]
                    s = lax.dot_general(
                        qx[h], kvt, (((1,), (1,)), ((), ())), preferred_element_type=jnp.float32
                    )
                    s = jnp.where(allowed, s, neg_big)
                    m_new = jnp.maximum(m, jnp.max(s, axis=1)[:, None])
                    p_w = jnp.exp(s - jnp.tile(m_new, (1, TK // LANES)))
                    alpha = jnp.exp(m - m_new)
                    pb = p_w.astype(jnp.bfloat16)
                    rhs = jnp.concatenate([kvt, ones], axis=1)
                    acc = jnp.tile(alpha, (1, 2)) * acc + jnp.dot(
                        pb, rhs, preferred_element_type=jnp.float32
                    )
                    new.append((m_new, acc))
                return tuple(new)

            carry = lax.fori_loop(lo_ref[base], hi_ref[base], body, carry)
        if finalize:
            for h in range(heads):
                m, acc = carry[h]
                outs[0][h] = (acc[:, HD:LANES] / acc[:, LANES + HD :]).astype(outs[0].dtype)
        else:
            for h in range(heads):
                m, acc = carry[h]
                outs[0][h] = m
                outs[1][h] = acc

    return kernel


def attend(q_h, q_scene, pieces, lo, hi, state):
    heads, qlen, _ = q_h.shape
    nq = qlen // TQ
    piece_rows = [kv.shape[1] for kv, _ in pieces]
    has_state = state is not None
    finalize = has_state
    kernel = make_kernel(piece_rows, heads, nq, has_state, finalize)
    in_specs = [
        pl.BlockSpec((heads, TQ, HD), lambda i, *_: (0, i, 0)),
        pl.BlockSpec((TQ, LANES), lambda i, *_: (i, 0)),
    ]
    args = [q_h, q_scene]
    for kv, ks in pieces:
        rows = kv.shape[1]
        in_specs.append(pl.BlockSpec((heads, rows, LANES), lambda i, *_: (0, 0, 0)))
        in_specs.append(pl.BlockSpec((1, rows), lambda i, *_: (0, 0)))
        args += [kv, ks]
    state_specs = [
        pl.BlockSpec((heads, TQ, w), lambda i, *_: (0, i, 0)) for w in (LANES, 2 * LANES)
    ]
    state_shapes = [
        jax.ShapeDtypeStruct((heads, qlen, w), jnp.float32) for w in (LANES, 2 * LANES)
    ]
    if has_state:
        in_specs += state_specs
        args += list(state)
    if finalize:
        out_specs = [pl.BlockSpec((heads, TQ, HD), lambda i, *_: (0, i, 0))]
        out_shape = [jax.ShapeDtypeStruct((heads, qlen, HD), jnp.bfloat16)]
    else:
        out_specs = state_specs
        out_shape = state_shapes
    return pl.pallas_call(
        kernel,
        out_shape=out_shape,
        grid_spec=pltpu.PrefetchScalarGridSpec(
            num_scalar_prefetch=2,
            grid=(nq,),
            in_specs=in_specs,
            out_specs=out_specs,
        ),
        compiler_params=pltpu.CompilerParams(dimension_semantics=("arbitrary",)),
    )(lo, hi, *args)


def local(queries, keys, values, coords, lengths):
    tok_dev, all_cols = queries.shape
    head_count = lax.axis_size("head")
    seq_count = lax.axis_size("seq")
    head_cols = all_cols // head_count
    local_heads = head_cols // HD
    group_len = tok_dev * head_count
    total_len = group_len * seq_count
    near = min(MOST, group_len)
    far = MOST - near

    def head_major(x):
        width = x.shape[-1]
        return x.reshape(tok_dev, head_count, local_heads, width).transpose(1, 2, 0, 3)

    angles = rotary_angles(coords)
    q_rot = head_major(rotate_rows(queries, angles, score_scale).astype(jnp.bfloat16))
    k_rot = rotate_rows(keys, angles).astype(jnp.bfloat16)
    v_rows = values.reshape(tok_dev, -1, HD)
    kv_src = head_major(jnp.concatenate([k_rot, v_rows], axis=-1))
    kv = lax.all_to_all(kv_src, "head", split_axis=0, concat_axis=2, tiled=True)
    kv = kv.reshape(local_heads, group_len, 2 * HD)
    q_h = lax.all_to_all(q_rot, "head", split_axis=0, concat_axis=2, tiled=True)
    q_h = q_h.reshape(local_heads, group_len, HD)

    below1 = shifted(kv, "seq", 1)
    above1 = shifted(kv, "seq", -1)
    halo = [(below1, -group_len), (above1, group_len)]
    if far > 0:
        below2 = shifted(kv[:, group_len - far :], "seq", 2)
        above2 = shifted(kv[:, :far], "seq", -2)
        halo = [(below2, -group_len - far)] + halo + [(above2, 2 * group_len)]

    own_start = lax.axis_index("seq") * group_len
    scene_end = jnp.cumsum(lengths).astype(jnp.int32)
    scene_begin = scene_end - lengths
    q_pos = own_start + jnp.arange(group_len, dtype=jnp.int32)
    q_scene = scene_of(q_pos, scene_end)
    first_scene = q_scene[::TQ]
    last_scene = q_scene[TQ - 1 :: TQ]
    span_lo = jnp.take(scene_begin, first_scene)
    span_hi = jnp.take(scene_end, last_scene)

    def tables(piece_list):
        los, his, prepared = [], [], []
        for kvp, offset in piece_list:
            rows = kvp.shape[1]
            p0 = own_start + offset
            k_pos = p0 + jnp.arange(rows, dtype=jnp.int32)
            k_valid = (k_pos >= 0) & (k_pos < total_len)
            k_scene = jnp.where(k_valid, scene_of(k_pos, scene_end), -1).astype(jnp.int32)
            lo = jnp.clip(span_lo - p0, 0, rows)
            hi = jnp.clip(span_hi - p0, 0, rows)
            klo = lo // TK
            khi = jnp.maximum((hi + TK - 1) // TK, klo)
            los.append(klo)
            his.append(khi)
            prepared.append((kvp, k_scene.reshape(1, rows)))
        return (
            jnp.concatenate(los).astype(jnp.int32),
            jnp.concatenate(his).astype(jnp.int32),
            prepared,
        )

    q_scene_col = jnp.broadcast_to(q_scene.astype(jnp.int32)[:, None], (group_len, LANES))
    lo0, hi0, prep0 = tables([(kv, 0)])
    state = attend(q_h, q_scene_col, prep0, lo0, hi0, None)
    lo1, hi1, prep1 = tables(halo)
    out_h = attend(q_h, q_scene_col, prep1, lo1, hi1, state)[0]

    out_src = out_h.reshape(local_heads, head_count, tok_dev, HD)
    back = lax.all_to_all(out_src, "head", split_axis=1, concat_axis=0, tiled=True)
    back = back.reshape(head_count * local_heads, tok_dev, HD)
    return back.transpose(1, 0, 2).reshape(tok_dev, all_cols)


def solution(mesh):
    in_specs = (
        P(("dp", "seq", "head"), None),
        P(("dp", "seq", "head"), None),
        P(("dp", "seq", "head"), None),
        P(None, ("dp", "seq", "head")),
        P("dp"),
    )
    out_specs = P(("dp", "seq", "head"), None)
    return jax.shard_map(local, mesh=mesh, in_specs=in_specs, out_specs=out_specs, check_vma=False)
```

```python
import jax
import jax.numpy as jnp
from jax import lax
from jax.experimental import pallas as pl
from jax.experimental.pallas import tpu as pltpu
from jax.sharding import PartitionSpec as P

HD = 64
MOST = 1536

score_scale = 0.125
neg_big = -1e30

TQ = 256
TK = 512


def shifted(block, axis, distance):
    devices = range(lax.axis_size(axis))
    route = [(i - distance, i) for i in devices if i - distance in devices]
    return lax.ppermute(block, axis, route)


def rotary_angles(coords):
    pair_count = HD // 2
    pair_id = jnp.arange(pair_count, dtype=jnp.int32)
    axis_of = 3 * pair_id // pair_count
    exponent = (3 * pair_id % pair_count).astype(jnp.float32) / pair_count
    frequency = jnp.power(jnp.float32(100.0), -exponent)
    position = coords.astype(jnp.float32)
    angles = jnp.zeros((coords.shape[1], pair_count), jnp.float32)
    for axis_id in range(3):
        picked = jnp.where(axis_of == axis_id, frequency, jnp.float32(0.0))
        angles = angles + position[axis_id][:, None] * picked[None, :]
    return angles


def rotate_rows(source, angles, scale=None):
    row_count = source.shape[0]
    per_head = source.reshape(row_count, -1, HD).astype(jnp.float32)
    half_size = HD // 2
    front_half = per_head[..., :half_size]
    back_half = per_head[..., half_size:]
    cos_val = jnp.cos(angles)[:, None, :]
    sin_val = jnp.sin(angles)[:, None, :]
    turned = jnp.concatenate(
        [front_half * cos_val - back_half * sin_val, front_half * sin_val + back_half * cos_val],
        axis=-1,
    )
    if scale is not None:
        turned = turned * jnp.float32(scale)
    return turned


def scene_of(positions, scene_end):
    return jnp.sum((positions[:, None] >= scene_end[None, :]).astype(jnp.int32), axis=1)


LANES = 128


def make_kernel(piece_rows, heads, nq, has_state, finalize):
    n_pieces = len(piece_rows)

    def kernel(lo_ref, hi_ref, q_ref, qs_ref, *rest):
        piece_refs = rest[: 2 * n_pieces]
        rest = rest[2 * n_pieces :]
        if has_state:
            m_in, acc_in = rest[:2]
            rest = rest[2:]
        outs = rest
        i = pl.program_id(0)
        tq = q_ref.shape[1]
        pad = jnp.zeros((tq, LANES - HD), jnp.bfloat16)
        qx = [jnp.concatenate([q_ref[h], pad], axis=1) for h in range(heads)]
        qs = jnp.tile(qs_ref[...], (1, TK // LANES))
        ones = jnp.ones((TK, LANES), jnp.bfloat16)
        two = 2 * LANES
        if has_state:
            carry = tuple((m_in[h], acc_in[h]) for h in range(heads))
        else:
            carry = tuple(
                (
                    jnp.full((tq, LANES), neg_big, jnp.float32),
                    jnp.zeros((tq, two), jnp.float32),
                )
                for h in range(heads)
            )
        for p in range(n_pieces):
            kv_ref, ks_ref = piece_refs[2 * p : 2 * p + 2]
            base = p * nq + i

            def body(j, carry, kv_ref=kv_ref, ks_ref=ks_ref):
                start = pl.multiple_of(j * TK, TK)
                allowed = qs == ks_ref[:, pl.ds(start, TK)]
                new = []
                for h in range(heads):
                    m, acc = carry[h]
                    kvt = kv_ref[h, pl.ds(start, TK), :]
                    s = lax.dot_general(
                        qx[h], kvt, (((1,), (1,)), ((), ())), preferred_element_type=jnp.float32
                    )
                    s = jnp.where(allowed, s, neg_big)
                    m_new = jnp.maximum(m, jnp.max(s, axis=1)[:, None])
                    p_w = jnp.exp(s - jnp.tile(m_new, (1, TK // LANES)))
                    alpha = jnp.exp(m - m_new)
                    pb = p_w.astype(jnp.bfloat16)
                    rhs = jnp.concatenate([kvt, ones], axis=1)
                    acc = jnp.tile(alpha, (1, 2)) * acc + jnp.dot(
                        pb, rhs, preferred_element_type=jnp.float32
                    )
                    new.append((m_new, acc))
                return tuple(new)

            carry = lax.fori_loop(lo_ref[base], hi_ref[base], body, carry)
        if finalize:
            for h in range(heads):
                m, acc = carry[h]
                outs[0][h] = (acc[:, HD:LANES] / acc[:, LANES + HD :]).astype(outs[0].dtype)
        else:
            for h in range(heads):
                m, acc = carry[h]
                outs[0][h] = m
                outs[1][h] = acc

    return kernel


def attend(q_h, q_scene, pieces, lo, hi, state, finalize):
    heads, qlen, _ = q_h.shape
    nq = qlen // TQ
    piece_rows = [kv.shape[1] for kv, _ in pieces]
    has_state = state is not None
    kernel = make_kernel(piece_rows, heads, nq, has_state, finalize)
    in_specs = [
        pl.BlockSpec((heads, TQ, HD), lambda i, *_: (0, i, 0)),
        pl.BlockSpec((TQ, LANES), lambda i, *_: (i, 0)),
    ]
    args = [q_h, q_scene]
    for kv, ks in pieces:
        rows = kv.shape[1]
        in_specs.append(pl.BlockSpec((heads, rows, LANES), lambda i, *_: (0, 0, 0)))
        in_specs.append(pl.BlockSpec((1, rows), lambda i, *_: (0, 0)))
        args += [kv, ks]
    state_specs = [
        pl.BlockSpec((heads, TQ, w), lambda i, *_: (0, i, 0)) for w in (LANES, 2 * LANES)
    ]
    state_shapes = [
        jax.ShapeDtypeStruct((heads, qlen, w), jnp.float32) for w in (LANES, 2 * LANES)
    ]
    if has_state:
        in_specs += state_specs
        args += list(state)
    if finalize:
        out_specs = [pl.BlockSpec((heads, TQ, HD), lambda i, *_: (0, i, 0))]
        out_shape = [jax.ShapeDtypeStruct((heads, qlen, HD), jnp.bfloat16)]
    else:
        out_specs = state_specs
        out_shape = state_shapes
    return pl.pallas_call(
        kernel,
        out_shape=out_shape,
        grid_spec=pltpu.PrefetchScalarGridSpec(
            num_scalar_prefetch=2,
            grid=(nq,),
            in_specs=in_specs,
            out_specs=out_specs,
        ),
        compiler_params=pltpu.CompilerParams(dimension_semantics=("arbitrary",)),
    )(lo, hi, *args)


def local(queries, keys, values, coords, lengths):
    tok_dev, all_cols = queries.shape
    head_count = lax.axis_size("head")
    seq_count = lax.axis_size("seq")
    head_cols = all_cols // head_count
    local_heads = head_cols // HD
    group_len = tok_dev * head_count
    total_len = group_len * seq_count
    near = min(MOST, group_len)
    far = MOST - near

    def head_major(x):
        width = x.shape[-1]
        return x.reshape(tok_dev, head_count, local_heads, width).transpose(1, 2, 0, 3)

    angles = rotary_angles(coords)
    q_rot = head_major(rotate_rows(queries, angles, score_scale).astype(jnp.bfloat16))
    k_rot = rotate_rows(keys, angles).astype(jnp.bfloat16)
    v_rows = values.reshape(tok_dev, -1, HD)
    kv_src = head_major(jnp.concatenate([k_rot, v_rows], axis=-1))
    kv = lax.all_to_all(kv_src, "head", split_axis=0, concat_axis=2, tiled=True)
    kv = kv.reshape(local_heads, group_len, 2 * HD)
    q_h = lax.all_to_all(q_rot, "head", split_axis=0, concat_axis=2, tiled=True)
    q_h = q_h.reshape(local_heads, group_len, HD)

    half = group_len - far
    below_hi = shifted(kv[:, half:], "seq", 1)
    below_lo = shifted(kv[:, :half], "seq", 1)
    above_lo = shifted(kv[:, :far], "seq", -1)
    above_hi = shifted(kv[:, far:], "seq", -1)
    near_pieces = [
        (below_lo, -group_len),
        (below_hi, -far),
        (above_lo, group_len),
        (above_hi, group_len + far),
    ]
    far_pieces = []
    if far > 0:
        below2 = shifted(below_hi, "seq", 1)
        above2 = shifted(above_lo, "seq", -1)
        far_pieces = [(below2, -group_len - far), (above2, 2 * group_len)]

    own_start = lax.axis_index("seq") * group_len
    scene_end = jnp.cumsum(lengths).astype(jnp.int32)
    scene_begin = scene_end - lengths
    q_pos = own_start + jnp.arange(group_len, dtype=jnp.int32)
    q_scene = scene_of(q_pos, scene_end)
    first_scene = q_scene[::TQ]
    last_scene = q_scene[TQ - 1 :: TQ]
    span_lo = jnp.take(scene_begin, first_scene)
    span_hi = jnp.take(scene_end, last_scene)

    def tables(piece_list):
        los, his, prepared = [], [], []
        for kvp, offset in piece_list:
            rows = kvp.shape[1]
            p0 = own_start + offset
            k_pos = p0 + jnp.arange(rows, dtype=jnp.int32)
            k_valid = (k_pos >= 0) & (k_pos < total_len)
            k_scene = jnp.where(k_valid, scene_of(k_pos, scene_end), -1).astype(jnp.int32)
            lo = jnp.clip(span_lo - p0, 0, rows)
            hi = jnp.clip(span_hi - p0, 0, rows)
            klo = lo // TK
            khi = jnp.maximum((hi + TK - 1) // TK, klo)
            los.append(klo)
            his.append(khi)
            prepared.append((kvp, k_scene.reshape(1, rows)))
        return (
            jnp.concatenate(los).astype(jnp.int32),
            jnp.concatenate(his).astype(jnp.int32),
            prepared,
        )

    q_scene_col = jnp.broadcast_to(q_scene.astype(jnp.int32)[:, None], (group_len, LANES))
    lo0, hi0, prep0 = tables([(kv, 0)])
    state = attend(q_h, q_scene_col, prep0, lo0, hi0, None, False)
    if far_pieces:
        lo1, hi1, prep1 = tables(near_pieces)
        state = attend(q_h, q_scene_col, prep1, lo1, hi1, state, False)
        lo2, hi2, prep2 = tables(far_pieces)
        out_h = attend(q_h, q_scene_col, prep2, lo2, hi2, state, True)[0]
    else:
        lo1, hi1, prep1 = tables(near_pieces)
        out_h = attend(q_h, q_scene_col, prep1, lo1, hi1, state, True)[0]

    out_src = out_h.reshape(local_heads, head_count, tok_dev, HD)
    back = lax.all_to_all(out_src, "head", split_axis=1, concat_axis=0, tiled=True)
    back = back.reshape(head_count * local_heads, tok_dev, HD)
    return back.transpose(1, 0, 2).reshape(tok_dev, all_cols)


def solution(mesh):
    in_specs = (
        P(("dp", "seq", "head"), None),
        P(("dp", "seq", "head"), None),
        P(("dp", "seq", "head"), None),
        P(None, ("dp", "seq", "head")),
        P("dp"),
    )
    out_specs = P(("dp", "seq", "head"), None)
    return jax.shard_map(local, mesh=mesh, in_specs=in_specs, out_specs=out_specs, check_vma=False)
```

```python
import jax
import jax.numpy as jnp
from jax import lax
from jax.experimental import pallas as pl
from jax.experimental.pallas import tpu as pltpu
from jax.sharding import PartitionSpec as P

HD = 64
MOST = 1536

score_scale = 0.125
neg_big = -1e30

TQ = 256
TK = 512


def shifted(block, axis, distance):
    devices = range(lax.axis_size(axis))
    route = [(i - distance, i) for i in devices if i - distance in devices]
    return lax.ppermute(block, axis, route)


def rotary_angles(coords):
    pair_count = HD // 2
    pair_id = jnp.arange(pair_count, dtype=jnp.int32)
    axis_of = 3 * pair_id // pair_count
    exponent = (3 * pair_id % pair_count).astype(jnp.float32) / pair_count
    frequency = jnp.power(jnp.float32(100.0), -exponent)
    position = coords.astype(jnp.float32)
    angles = jnp.zeros((coords.shape[1], pair_count), jnp.float32)
    for axis_id in range(3):
        picked = jnp.where(axis_of == axis_id, frequency, jnp.float32(0.0))
        angles = angles + position[axis_id][:, None] * picked[None, :]
    return angles


def rotate_rows(source, angles, scale=None):
    row_count = source.shape[0]
    per_head = source.reshape(row_count, -1, HD).astype(jnp.float32)
    half_size = HD // 2
    front_half = per_head[..., :half_size]
    back_half = per_head[..., half_size:]
    cos_val = jnp.cos(angles)[:, None, :]
    sin_val = jnp.sin(angles)[:, None, :]
    turned = jnp.concatenate(
        [front_half * cos_val - back_half * sin_val, front_half * sin_val + back_half * cos_val],
        axis=-1,
    )
    if scale is not None:
        turned = turned * jnp.float32(scale)
    return turned


def scene_of(positions, scene_end):
    return jnp.sum((positions[:, None] >= scene_end[None, :]).astype(jnp.int32), axis=1)


LANES = 128


def make_kernel(piece_rows, heads, nq, has_state, finalize):
    n_pieces = len(piece_rows)

    def kernel(lo_ref, hi_ref, q_ref, qs_ref, *rest):
        piece_refs = rest[: 2 * n_pieces]
        rest = rest[2 * n_pieces :]
        if has_state:
            m_in, acc_in = rest[:2]
            rest = rest[2:]
        outs = rest
        i = pl.program_id(0)
        tq = q_ref.shape[1]
        pad = jnp.zeros((tq, LANES - HD), jnp.bfloat16)
        qx = [jnp.concatenate([q_ref[h], pad], axis=1) for h in range(heads)]
        qs = jnp.tile(qs_ref[...], (1, TK // LANES))
        ones = jnp.ones((TK, LANES), jnp.bfloat16)
        two = 2 * LANES
        if has_state:
            carry = tuple((m_in[h], acc_in[h]) for h in range(heads))
        else:
            carry = tuple(
                (
                    jnp.full((tq, LANES), neg_big, jnp.float32),
                    jnp.zeros((tq, two), jnp.float32),
                )
                for h in range(heads)
            )
        for p in range(n_pieces):
            kv_ref, ks_ref = piece_refs[2 * p : 2 * p + 2]
            base = p * nq + i

            def body(j, carry, kv_ref=kv_ref, ks_ref=ks_ref):
                start = pl.multiple_of(j * TK, TK)
                allowed = qs == ks_ref[:, pl.ds(start, TK)]
                new = []
                for h in range(heads):
                    m, acc = carry[h]
                    kvt = kv_ref[h, pl.ds(start, TK), :]
                    s = lax.dot_general(
                        qx[h], kvt, (((1,), (1,)), ((), ())), preferred_element_type=jnp.float32
                    )
                    s = jnp.where(allowed, s, neg_big)
                    m_new = jnp.maximum(m, jnp.max(s, axis=1)[:, None])
                    p_w = jnp.exp(s - jnp.tile(m_new, (1, TK // LANES)))
                    alpha = jnp.exp(m - m_new)
                    pb = p_w.astype(jnp.bfloat16)
                    rhs = jnp.concatenate([kvt, ones], axis=1)
                    acc = jnp.tile(alpha, (1, 2)) * acc + jnp.dot(
                        pb, rhs, preferred_element_type=jnp.float32
                    )
                    new.append((m_new, acc))
                return tuple(new)

            carry = lax.fori_loop(lo_ref[base], hi_ref[base], body, carry)
        if finalize:
            for h in range(heads):
                m, acc = carry[h]
                outs[0][h] = (acc[:, HD:LANES] / acc[:, LANES + HD :]).astype(outs[0].dtype)
        else:
            for h in range(heads):
                m, acc = carry[h]
                outs[0][h] = m
                outs[1][h] = acc

    return kernel


def attend(q_h, q_scene, pieces, lo, hi, state, finalize, group=None):
    heads, qlen, _ = q_h.shape
    g = 0
    if group is not None:
        g, heads = group
    nq = qlen // TQ
    piece_rows = [kv.shape[1] for kv, _ in pieces]
    has_state = state is not None
    kernel = make_kernel(piece_rows, heads, nq, has_state, finalize)
    in_specs = [
        pl.BlockSpec((heads, TQ, HD), lambda i, *_: (g, i, 0)),
        pl.BlockSpec((TQ, LANES), lambda i, *_: (i, 0)),
    ]
    args = [q_h, q_scene]
    for kv, ks in pieces:
        rows = kv.shape[1]
        in_specs.append(pl.BlockSpec((heads, rows, LANES), lambda i, *_: (g, 0, 0)))
        in_specs.append(pl.BlockSpec((1, rows), lambda i, *_: (0, 0)))
        args += [kv, ks]
    state_specs = [
        pl.BlockSpec((heads, TQ, w), lambda i, *_: (0, i, 0)) for w in (LANES, 2 * LANES)
    ]
    in_state_specs = [
        pl.BlockSpec((heads, TQ, w), lambda i, *_: (g, i, 0)) for w in (LANES, 2 * LANES)
    ]
    state_shapes = [
        jax.ShapeDtypeStruct((heads, qlen, w), jnp.float32) for w in (LANES, 2 * LANES)
    ]
    if has_state:
        in_specs += in_state_specs
        args += list(state)
    if finalize:
        out_specs = [pl.BlockSpec((heads, TQ, HD), lambda i, *_: (0, i, 0))]
        out_shape = [jax.ShapeDtypeStruct((heads, qlen, HD), jnp.bfloat16)]
    else:
        out_specs = state_specs
        out_shape = state_shapes
    return pl.pallas_call(
        kernel,
        out_shape=out_shape,
        grid_spec=pltpu.PrefetchScalarGridSpec(
            num_scalar_prefetch=2,
            grid=(nq,),
            in_specs=in_specs,
            out_specs=out_specs,
        ),
        compiler_params=pltpu.CompilerParams(dimension_semantics=("arbitrary",)),
    )(lo, hi, *args)


def local(queries, keys, values, coords, lengths):
    tok_dev, all_cols = queries.shape
    head_count = lax.axis_size("head")
    seq_count = lax.axis_size("seq")
    head_cols = all_cols // head_count
    local_heads = head_cols // HD
    group_len = tok_dev * head_count
    total_len = group_len * seq_count
    near = min(MOST, group_len)
    far = MOST - near

    def head_major(x):
        width = x.shape[-1]
        return x.reshape(tok_dev, head_count, local_heads, width).transpose(1, 2, 0, 3)

    angles = rotary_angles(coords)
    q_rot = head_major(rotate_rows(queries, angles, score_scale).astype(jnp.bfloat16))
    k_rot = rotate_rows(keys, angles).astype(jnp.bfloat16)
    v_rows = values.reshape(tok_dev, -1, HD)
    kv_src = head_major(jnp.concatenate([k_rot, v_rows], axis=-1))
    kv = lax.all_to_all(kv_src, "head", split_axis=0, concat_axis=2, tiled=True)
    kv = kv.reshape(local_heads, group_len, 2 * HD)
    q_h = lax.all_to_all(q_rot, "head", split_axis=0, concat_axis=2, tiled=True)
    q_h = q_h.reshape(local_heads, group_len, HD)

    half = group_len - far
    below_hi = shifted(kv[:, half:], "seq", 1)
    below_lo = shifted(kv[:, :half], "seq", 1)
    above_lo = shifted(kv[:, :far], "seq", -1)
    above_hi = shifted(kv[:, far:], "seq", -1)
    near_pieces = [
        (below_lo, -group_len),
        (below_hi, -far),
        (above_lo, group_len),
        (above_hi, group_len + far),
    ]
    far_pieces = []
    if far > 0:
        below2 = shifted(below_hi, "seq", 1)
        above2 = shifted(above_lo, "seq", -1)
        far_pieces = [(below2, -group_len - far), (above2, 2 * group_len)]

    own_start = lax.axis_index("seq") * group_len
    scene_end = jnp.cumsum(lengths).astype(jnp.int32)
    scene_begin = scene_end - lengths
    q_pos = own_start + jnp.arange(group_len, dtype=jnp.int32)
    q_scene = scene_of(q_pos, scene_end)
    first_scene = q_scene[::TQ]
    last_scene = q_scene[TQ - 1 :: TQ]
    span_lo = jnp.take(scene_begin, first_scene)
    span_hi = jnp.take(scene_end, last_scene)

    def tables(piece_list):
        los, his, prepared = [], [], []
        for kvp, offset in piece_list:
            rows = kvp.shape[1]
            p0 = own_start + offset
            k_pos = p0 + jnp.arange(rows, dtype=jnp.int32)
            k_valid = (k_pos >= 0) & (k_pos < total_len)
            k_scene = jnp.where(k_valid, scene_of(k_pos, scene_end), -1).astype(jnp.int32)
            lo = jnp.clip(span_lo - p0, 0, rows)
            hi = jnp.clip(span_hi - p0, 0, rows)
            klo = lo // TK
            khi = jnp.maximum((hi + TK - 1) // TK, klo)
            los.append(klo)
            his.append(khi)
            prepared.append((kvp, k_scene.reshape(1, rows)))
        return (
            jnp.concatenate(los).astype(jnp.int32),
            jnp.concatenate(his).astype(jnp.int32),
            prepared,
        )

    q_scene_col = jnp.broadcast_to(q_scene.astype(jnp.int32)[:, None], (group_len, LANES))
    lo0, hi0, prep0 = tables([(kv, 0)])
    state = attend(q_h, q_scene_col, prep0, lo0, hi0, None, False)
    lo1, hi1, prep1 = tables(near_pieces)
    if far_pieces:
        state = attend(q_h, q_scene_col, prep1, lo1, hi1, state, False)
        lo2, hi2, prep2 = tables(far_pieces)
        last = (lo2, hi2, prep2)
    else:
        last = (lo1, hi1, prep1)
    split = 2 if local_heads % 2 == 0 else 1
    part_heads = local_heads // split
    returned = []
    for g in range(split):
        out_g = attend(q_h, q_scene_col, last[2], last[0], last[1], state, True, (g, part_heads))[0]
        out_src = out_g.reshape(part_heads, head_count, tok_dev, HD)
        back = lax.all_to_all(out_src, "head", split_axis=1, concat_axis=0, tiled=True)
        returned.append(back.reshape(head_count, part_heads, tok_dev, HD))
    back = jnp.stack(returned, axis=1).reshape(head_count * local_heads, tok_dev, HD)
    return back.transpose(1, 0, 2).reshape(tok_dev, all_cols)


def solution(mesh):
    in_specs = (
        P(("dp", "seq", "head"), None),
        P(("dp", "seq", "head"), None),
        P(("dp", "seq", "head"), None),
        P(None, ("dp", "seq", "head")),
        P("dp"),
    )
    out_specs = P(("dp", "seq", "head"), None)
    return jax.shard_map(local, mesh=mesh, in_specs=in_specs, out_specs=out_specs, check_vma=False)
```

```python
import jax
import jax.numpy as jnp
from jax import lax
from jax.experimental import pallas as pl
from jax.experimental.pallas import tpu as pltpu
from jax.sharding import PartitionSpec as P

HD = 64
MOST = 1536

score_scale = 0.125
neg_big = -1e30

TQ = 256
TK = 512


def shifted(block, axis, distance):
    devices = range(lax.axis_size(axis))
    route = [(i - distance, i) for i in devices if i - distance in devices]
    return lax.ppermute(block, axis, route)


def rotary_angles(coords):
    pair_count = HD // 2
    pair_id = jnp.arange(pair_count, dtype=jnp.int32)
    axis_of = 3 * pair_id // pair_count
    exponent = (3 * pair_id % pair_count).astype(jnp.float32) / pair_count
    frequency = jnp.power(jnp.float32(100.0), -exponent)
    position = coords.astype(jnp.float32)
    angles = jnp.zeros((coords.shape[1], pair_count), jnp.float32)
    for axis_id in range(3):
        picked = jnp.where(axis_of == axis_id, frequency, jnp.float32(0.0))
        angles = angles + position[axis_id][:, None] * picked[None, :]
    return angles


def rotate_rows(source, angles, scale=None):
    row_count = source.shape[0]
    per_head = source.reshape(row_count, -1, HD).astype(jnp.float32)
    half_size = HD // 2
    front_half = per_head[..., :half_size]
    back_half = per_head[..., half_size:]
    cos_val = jnp.cos(angles)[:, None, :]
    sin_val = jnp.sin(angles)[:, None, :]
    turned = jnp.concatenate(
        [front_half * cos_val - back_half * sin_val, front_half * sin_val + back_half * cos_val],
        axis=-1,
    )
    if scale is not None:
        turned = turned * jnp.float32(scale)
    return turned


def scene_of(positions, scene_end):
    return jnp.sum((positions[:, None] >= scene_end[None, :]).astype(jnp.int32), axis=1)


LANES = 128


def make_kernel(piece_rows, heads, nq, has_state, finalize):
    n_pieces = len(piece_rows)

    def kernel(lo_ref, hi_ref, q_ref, qs_ref, *rest):
        piece_refs = rest[: 2 * n_pieces]
        rest = rest[2 * n_pieces :]
        if has_state:
            m_in, acc_in = rest[:2]
            rest = rest[2:]
        outs = rest
        i = pl.program_id(0)
        tq = q_ref.shape[1]
        pad = jnp.zeros((tq, LANES - HD), jnp.bfloat16)
        qx = [jnp.concatenate([q_ref[h], pad], axis=1) for h in range(heads)]
        qs = jnp.tile(qs_ref[...], (1, TK // LANES))
        ones = jnp.ones((TK, LANES), jnp.bfloat16)
        two = 2 * LANES
        if has_state:
            carry = tuple((m_in[h], acc_in[h]) for h in range(heads))
        else:
            carry = tuple(
                (
                    jnp.full((tq, LANES), neg_big, jnp.float32),
                    jnp.zeros((tq, two), jnp.float32),
                )
                for h in range(heads)
            )
        for p in range(n_pieces):
            kv_ref, ks_ref = piece_refs[2 * p : 2 * p + 2]
            base = p * nq + i

            def body(j, carry, kv_ref=kv_ref, ks_ref=ks_ref):
                start = pl.multiple_of(j * TK, TK)
                allowed = qs == ks_ref[:, pl.ds(start, TK)]
                new = []
                for h in range(heads):
                    m, acc = carry[h]
                    kvt = kv_ref[h, pl.ds(start, TK), :]
                    s = lax.dot_general(
                        qx[h], kvt, (((1,), (1,)), ((), ())), preferred_element_type=jnp.float32
                    )
                    s = jnp.where(allowed, s, neg_big)
                    m_new = jnp.maximum(m, jnp.max(s, axis=1)[:, None])
                    p_w = jnp.exp(s - jnp.tile(m_new, (1, TK // LANES)))
                    alpha = jnp.exp(m - m_new)
                    pb = p_w.astype(jnp.bfloat16)
                    rhs = jnp.concatenate([kvt, ones], axis=1)
                    acc = jnp.tile(alpha, (1, 2)) * acc + jnp.dot(
                        pb, rhs, preferred_element_type=jnp.float32
                    )
                    new.append((m_new, acc))
                return tuple(new)

            carry = lax.fori_loop(lo_ref[base], hi_ref[base], body, carry)
        if finalize:
            for h in range(heads):
                m, acc = carry[h]
                outs[0][h] = (acc[:, HD:LANES] / acc[:, LANES + HD :]).astype(outs[0].dtype)
        else:
            for h in range(heads):
                m, acc = carry[h]
                outs[0][h] = m
                outs[1][h] = acc

    return kernel


def attend(q_h, q_scene, pieces, lo, hi, state, finalize):
    heads, qlen, _ = q_h.shape
    nq = qlen // TQ
    piece_rows = [kv.shape[1] for kv, _ in pieces]
    has_state = state is not None
    kernel = make_kernel(piece_rows, heads, nq, has_state, finalize)
    in_specs = [
        pl.BlockSpec((heads, TQ, HD), lambda i, *_: (0, i, 0)),
        pl.BlockSpec((TQ, LANES), lambda i, *_: (i, 0)),
    ]
    args = [q_h, q_scene]
    for kv, ks in pieces:
        rows = kv.shape[1]
        in_specs.append(pl.BlockSpec((heads, rows, LANES), lambda i, *_: (0, 0, 0)))
        in_specs.append(pl.BlockSpec((1, rows), lambda i, *_: (0, 0)))
        args += [kv, ks]
    state_specs = [
        pl.BlockSpec((heads, TQ, w), lambda i, *_: (0, i, 0)) for w in (LANES, 2 * LANES)
    ]
    state_shapes = [
        jax.ShapeDtypeStruct((heads, qlen, w), jnp.float32) for w in (LANES, 2 * LANES)
    ]
    if has_state:
        in_specs += state_specs
        args += list(state)
    if finalize:
        out_specs = [pl.BlockSpec((heads, TQ, HD), lambda i, *_: (0, i, 0))]
        out_shape = [jax.ShapeDtypeStruct((heads, qlen, HD), jnp.bfloat16)]
    else:
        out_specs = state_specs
        out_shape = state_shapes
    return pl.pallas_call(
        kernel,
        out_shape=out_shape,
        grid_spec=pltpu.PrefetchScalarGridSpec(
            num_scalar_prefetch=2,
            grid=(nq,),
            in_specs=in_specs,
            out_specs=out_specs,
        ),
        compiler_params=pltpu.CompilerParams(dimension_semantics=("arbitrary",)),
    )(lo, hi, *args)


def local(queries, keys, values, coords, lengths):
    tok_dev, all_cols = queries.shape
    head_count = lax.axis_size("head")
    seq_count = lax.axis_size("seq")
    head_cols = all_cols // head_count
    local_heads = head_cols // HD
    group_len = tok_dev * head_count
    total_len = group_len * seq_count
    near = min(MOST, group_len)
    far = MOST - near

    def head_major(x):
        width = x.shape[-1]
        return x.reshape(tok_dev, head_count, local_heads, width).transpose(1, 2, 0, 3)

    angles = rotary_angles(coords)
    q_rot = head_major(rotate_rows(queries, angles, score_scale).astype(jnp.bfloat16))
    k_rot = rotate_rows(keys, angles).astype(jnp.bfloat16)
    v_rows = values.reshape(tok_dev, -1, HD)
    kv_src = head_major(jnp.concatenate([k_rot, v_rows], axis=-1))
    kv = lax.all_to_all(kv_src, "head", split_axis=0, concat_axis=2, tiled=True)
    kv = kv.reshape(local_heads, group_len, 2 * HD)
    q_h = lax.all_to_all(q_rot, "head", split_axis=0, concat_axis=2, tiled=True)
    q_h = q_h.reshape(local_heads, group_len, HD)

    half = group_len - far
    below_hi = shifted(kv[:, half:], "seq", 1)
    below_lo = shifted(kv[:, :half], "seq", 1)
    above_lo = shifted(kv[:, :far], "seq", -1)
    above_hi = shifted(kv[:, far:], "seq", -1)
    near_pieces = [
        (below_lo, -group_len),
        (below_hi, -far),
        (above_lo, group_len),
        (above_hi, group_len + far),
    ]
    far_pieces = []
    if far > 0:
        below2 = shifted(below_hi, "seq", 1)
        above2 = shifted(above_lo, "seq", -1)
        far_pieces = [(below2, -group_len - far), (above2, 2 * group_len)]

    own_start = lax.axis_index("seq") * group_len
    scene_end = jnp.cumsum(lengths).astype(jnp.int32)
    scene_begin = scene_end - lengths
    q_pos = own_start + jnp.arange(group_len, dtype=jnp.int32)
    q_scene = scene_of(q_pos, scene_end)
    first_scene = q_scene[::TQ]
    last_scene = q_scene[TQ - 1 :: TQ]
    span_lo = jnp.take(scene_begin, first_scene)
    span_hi = jnp.take(scene_end, last_scene)

    def tables(piece_list):
        los, his, prepared = [], [], []
        for kvp, offset in piece_list:
            rows = kvp.shape[1]
            p0 = own_start + offset
            k_pos = p0 + jnp.arange(rows, dtype=jnp.int32)
            k_valid = (k_pos >= 0) & (k_pos < total_len)
            k_scene = jnp.where(k_valid, scene_of(k_pos, scene_end), -1).astype(jnp.int32)
            lo = jnp.clip(span_lo - p0, 0, rows)
            hi = jnp.clip(span_hi - p0, 0, rows)
            klo = lo // TK
            khi = jnp.maximum((hi + TK - 1) // TK, klo)
            los.append(klo)
            his.append(khi)
            prepared.append((kvp, k_scene.reshape(1, rows)))
        return (
            jnp.concatenate(los).astype(jnp.int32),
            jnp.concatenate(his).astype(jnp.int32),
            prepared,
        )

    q_scene_col = jnp.broadcast_to(q_scene.astype(jnp.int32)[:, None], (group_len, LANES))
    if far_pieces:
        first = [(kv, 0), (below_hi, -far), (above_lo, group_len)]
        second = [(below_lo, -group_len), (above_hi, group_len + far)] + far_pieces
    else:
        first = [(kv, 0)]
        second = near_pieces
    lo0, hi0, prep0 = tables(first)
    state = attend(q_h, q_scene_col, prep0, lo0, hi0, None, False)
    lo1, hi1, prep1 = tables(second)
    out_h = attend(q_h, q_scene_col, prep1, lo1, hi1, state, True)[0]

    out_src = out_h.reshape(local_heads, head_count, tok_dev, HD)
    back = lax.all_to_all(out_src, "head", split_axis=1, concat_axis=0, tiled=True)
    back = back.reshape(head_count * local_heads, tok_dev, HD)
    return back.transpose(1, 0, 2).reshape(tok_dev, all_cols)


def solution(mesh):
    in_specs = (
        P(("dp", "seq", "head"), None),
        P(("dp", "seq", "head"), None),
        P(("dp", "seq", "head"), None),
        P(None, ("dp", "seq", "head")),
        P("dp"),
    )
    out_specs = P(("dp", "seq", "head"), None)
    return jax.shard_map(local, mesh=mesh, in_specs=in_specs, out_specs=out_specs, check_vma=False)
```

```python
import jax
import jax.numpy as jnp
from jax import lax
from jax.experimental import pallas as pl
from jax.experimental.pallas import tpu as pltpu
from jax.sharding import PartitionSpec as P

HD = 64
MOST = 1536

score_scale = 0.125
neg_big = -1e30

TQ = 256
TK = 512
TK_HALO = 256


def shifted(block, axis, distance):
    devices = range(lax.axis_size(axis))
    route = [(i - distance, i) for i in devices if i - distance in devices]
    return lax.ppermute(block, axis, route)


def rotary_angles(coords):
    pair_count = HD // 2
    pair_id = jnp.arange(pair_count, dtype=jnp.int32)
    axis_of = 3 * pair_id // pair_count
    exponent = (3 * pair_id % pair_count).astype(jnp.float32) / pair_count
    frequency = jnp.power(jnp.float32(100.0), -exponent)
    position = coords.astype(jnp.float32)
    angles = jnp.zeros((coords.shape[1], pair_count), jnp.float32)
    for axis_id in range(3):
        picked = jnp.where(axis_of == axis_id, frequency, jnp.float32(0.0))
        angles = angles + position[axis_id][:, None] * picked[None, :]
    return angles


def rotate_rows(source, angles, scale=None):
    row_count = source.shape[0]
    per_head = source.reshape(row_count, -1, HD).astype(jnp.float32)
    half_size = HD // 2
    front_half = per_head[..., :half_size]
    back_half = per_head[..., half_size:]
    cos_val = jnp.cos(angles)[:, None, :]
    sin_val = jnp.sin(angles)[:, None, :]
    turned = jnp.concatenate(
        [front_half * cos_val - back_half * sin_val, front_half * sin_val + back_half * cos_val],
        axis=-1,
    )
    if scale is not None:
        turned = turned * jnp.float32(scale)
    return turned


def scene_of(positions, scene_end):
    return jnp.sum((positions[:, None] >= scene_end[None, :]).astype(jnp.int32), axis=1)


LANES = 128


def make_kernel(piece_rows, heads, nq, has_state, finalize, TK):
    n_pieces = len(piece_rows)

    def kernel(lo_ref, hi_ref, q_ref, qs_ref, *rest):
        piece_refs = rest[: 2 * n_pieces]
        rest = rest[2 * n_pieces :]
        if has_state:
            m_in, acc_in = rest[:2]
            rest = rest[2:]
        outs = rest
        i = pl.program_id(0)
        tq = q_ref.shape[1]
        pad = jnp.zeros((tq, LANES - HD), jnp.bfloat16)
        qx = [jnp.concatenate([q_ref[h], pad], axis=1) for h in range(heads)]
        qs = jnp.tile(qs_ref[...], (1, TK // LANES))
        ones = jnp.ones((TK, LANES), jnp.bfloat16)
        two = 2 * LANES
        if has_state:
            carry = tuple((m_in[h], acc_in[h]) for h in range(heads))
        else:
            carry = tuple(
                (
                    jnp.full((tq, LANES), neg_big, jnp.float32),
                    jnp.zeros((tq, two), jnp.float32),
                )
                for h in range(heads)
            )
        for p in range(n_pieces):
            kv_ref, ks_ref = piece_refs[2 * p : 2 * p + 2]
            base = p * nq + i

            def body(j, carry, kv_ref=kv_ref, ks_ref=ks_ref):
                start = pl.multiple_of(j * TK, TK)
                allowed = qs == ks_ref[:, pl.ds(start, TK)]
                new = []
                for h in range(heads):
                    m, acc = carry[h]
                    kvt = kv_ref[h, pl.ds(start, TK), :]
                    s = lax.dot_general(
                        qx[h], kvt, (((1,), (1,)), ((), ())), preferred_element_type=jnp.float32
                    )
                    s = jnp.where(allowed, s, neg_big)
                    m_new = jnp.maximum(m, jnp.max(s, axis=1)[:, None])
                    p_w = jnp.exp(s - jnp.tile(m_new, (1, TK // LANES)))
                    alpha = jnp.exp(m - m_new)
                    pb = p_w.astype(jnp.bfloat16)
                    rhs = jnp.concatenate([kvt, ones], axis=1)
                    acc = jnp.tile(alpha, (1, 2)) * acc + jnp.dot(
                        pb, rhs, preferred_element_type=jnp.float32
                    )
                    new.append((m_new, acc))
                return tuple(new)

            carry = lax.fori_loop(lo_ref[base], hi_ref[base], body, carry)
        if finalize:
            for h in range(heads):
                m, acc = carry[h]
                outs[0][h] = (acc[:, HD:LANES] / acc[:, LANES + HD :]).astype(outs[0].dtype)
        else:
            for h in range(heads):
                m, acc = carry[h]
                outs[0][h] = m
                outs[1][h] = acc

    return kernel


def attend(q_h, q_scene, pieces, lo, hi, state, finalize, tk):
    heads, qlen, _ = q_h.shape
    nq = qlen // TQ
    piece_rows = [kv.shape[1] for kv, _ in pieces]
    has_state = state is not None
    kernel = make_kernel(piece_rows, heads, nq, has_state, finalize, tk)
    in_specs = [
        pl.BlockSpec((heads, TQ, HD), lambda i, *_: (0, i, 0)),
        pl.BlockSpec((TQ, LANES), lambda i, *_: (i, 0)),
    ]
    args = [q_h, q_scene]
    for kv, ks in pieces:
        rows = kv.shape[1]
        in_specs.append(pl.BlockSpec((heads, rows, LANES), lambda i, *_: (0, 0, 0)))
        in_specs.append(pl.BlockSpec((1, rows), lambda i, *_: (0, 0)))
        args += [kv, ks]
    state_specs = [
        pl.BlockSpec((heads, TQ, w), lambda i, *_: (0, i, 0)) for w in (LANES, 2 * LANES)
    ]
    state_shapes = [
        jax.ShapeDtypeStruct((heads, qlen, w), jnp.float32) for w in (LANES, 2 * LANES)
    ]
    if has_state:
        in_specs += state_specs
        args += list(state)
    if finalize:
        out_specs = [pl.BlockSpec((heads, TQ, HD), lambda i, *_: (0, i, 0))]
        out_shape = [jax.ShapeDtypeStruct((heads, qlen, HD), jnp.bfloat16)]
    else:
        out_specs = state_specs
        out_shape = state_shapes
    return pl.pallas_call(
        kernel,
        out_shape=out_shape,
        grid_spec=pltpu.PrefetchScalarGridSpec(
            num_scalar_prefetch=2,
            grid=(nq,),
            in_specs=in_specs,
            out_specs=out_specs,
        ),
        compiler_params=pltpu.CompilerParams(dimension_semantics=("arbitrary",)),
    )(lo, hi, *args)


def local(queries, keys, values, coords, lengths):
    tok_dev, all_cols = queries.shape
    head_count = lax.axis_size("head")
    seq_count = lax.axis_size("seq")
    head_cols = all_cols // head_count
    local_heads = head_cols // HD
    group_len = tok_dev * head_count
    total_len = group_len * seq_count
    near = min(MOST, group_len)
    far = MOST - near

    def head_major(x):
        width = x.shape[-1]
        return x.reshape(tok_dev, head_count, local_heads, width).transpose(1, 2, 0, 3)

    angles = rotary_angles(coords)
    q_rot = head_major(rotate_rows(queries, angles, score_scale).astype(jnp.bfloat16))
    k_rot = rotate_rows(keys, angles).astype(jnp.bfloat16)
    v_rows = values.reshape(tok_dev, -1, HD)
    kv_src = head_major(jnp.concatenate([k_rot, v_rows], axis=-1))
    kv = lax.all_to_all(kv_src, "head", split_axis=0, concat_axis=2, tiled=True)
    kv = kv.reshape(local_heads, group_len, 2 * HD)
    q_h = lax.all_to_all(q_rot, "head", split_axis=0, concat_axis=2, tiled=True)
    q_h = q_h.reshape(local_heads, group_len, HD)

    half = group_len - far
    below_hi = shifted(kv[:, half:], "seq", 1)
    below_lo = shifted(kv[:, :half], "seq", 1)
    above_lo = shifted(kv[:, :far], "seq", -1)
    above_hi = shifted(kv[:, far:], "seq", -1)
    near_pieces = [
        (below_lo, -group_len),
        (below_hi, -far),
        (above_lo, group_len),
        (above_hi, group_len + far),
    ]
    far_pieces = []
    if far > 0:
        below2 = shifted(below_hi, "seq", 1)
        above2 = shifted(above_lo, "seq", -1)
        far_pieces = [(below2, -group_len - far), (above2, 2 * group_len)]

    own_start = lax.axis_index("seq") * group_len
    scene_end = jnp.cumsum(lengths).astype(jnp.int32)
    scene_begin = scene_end - lengths
    q_pos = own_start + jnp.arange(group_len, dtype=jnp.int32)
    q_scene = scene_of(q_pos, scene_end)
    first_scene = q_scene[::TQ]
    last_scene = q_scene[TQ - 1 :: TQ]
    span_lo = jnp.take(scene_begin, first_scene)
    span_hi = jnp.take(scene_end, last_scene)

    def tables(piece_list, TK):
        los, his, prepared = [], [], []
        for kvp, offset in piece_list:
            rows = kvp.shape[1]
            p0 = own_start + offset
            k_pos = p0 + jnp.arange(rows, dtype=jnp.int32)
            k_valid = (k_pos >= 0) & (k_pos < total_len)
            k_scene = jnp.where(k_valid, scene_of(k_pos, scene_end), -1).astype(jnp.int32)
            lo = jnp.clip(span_lo - p0, 0, rows)
            hi = jnp.clip(span_hi - p0, 0, rows)
            klo = lo // TK
            khi = jnp.maximum((hi + TK - 1) // TK, klo)
            los.append(klo)
            his.append(khi)
            prepared.append((kvp, k_scene.reshape(1, rows)))
        return (
            jnp.concatenate(los).astype(jnp.int32),
            jnp.concatenate(his).astype(jnp.int32),
            prepared,
        )

    q_scene_col = jnp.broadcast_to(q_scene.astype(jnp.int32)[:, None], (group_len, LANES))
    if far_pieces:
        first = [(kv, 0), (below_hi, -far), (above_lo, group_len)]
        second = [(below_lo, -group_len), (above_hi, group_len + far)] + far_pieces
    else:
        first = [(kv, 0)]
        second = near_pieces
    lo0, hi0, prep0 = tables(first, TK)
    state = attend(q_h, q_scene_col, prep0, lo0, hi0, None, False, TK)
    lo1, hi1, prep1 = tables(second, TK_HALO)
    out_h = attend(q_h, q_scene_col, prep1, lo1, hi1, state, True, TK_HALO)[0]

    out_src = out_h.reshape(local_heads, head_count, tok_dev, HD)
    back = lax.all_to_all(out_src, "head", split_axis=1, concat_axis=0, tiled=True)
    back = back.reshape(head_count * local_heads, tok_dev, HD)
    return back.transpose(1, 0, 2).reshape(tok_dev, all_cols)


def solution(mesh):
    in_specs = (
        P(("dp", "seq", "head"), None),
        P(("dp", "seq", "head"), None),
        P(("dp", "seq", "head"), None),
        P(None, ("dp", "seq", "head")),
        P("dp"),
    )
    out_specs = P(("dp", "seq", "head"), None)
    return jax.shard_map(local, mesh=mesh, in_specs=in_specs, out_specs=out_specs, check_vma=False)
```

```python
import jax
import jax.numpy as jnp
from jax import lax
from jax.experimental import pallas as pl
from jax.experimental.pallas import tpu as pltpu
from jax.sharding import PartitionSpec as P

HD = 64
MOST = 1536

score_scale = 0.125
neg_big = -1e30

TQ = 256
TK = 512
TK_HALO = 256


def shifted(block, axis, distance):
    devices = range(lax.axis_size(axis))
    route = [(i - distance, i) for i in devices if i - distance in devices]
    return lax.ppermute(block, axis, route)


def rotary_angles(coords):
    pair_count = HD // 2
    pair_id = jnp.arange(pair_count, dtype=jnp.int32)
    axis_of = 3 * pair_id // pair_count
    exponent = (3 * pair_id % pair_count).astype(jnp.float32) / pair_count
    frequency = jnp.power(jnp.float32(100.0), -exponent)
    position = coords.astype(jnp.float32)
    angles = jnp.zeros((coords.shape[1], pair_count), jnp.float32)
    for axis_id in range(3):
        picked = jnp.where(axis_of == axis_id, frequency, jnp.float32(0.0))
        angles = angles + position[axis_id][:, None] * picked[None, :]
    return angles


def rotate_rows(source, angles, scale=None):
    row_count = source.shape[0]
    per_head = source.reshape(row_count, -1, HD).astype(jnp.float32)
    half_size = HD // 2
    front_half = per_head[..., :half_size]
    back_half = per_head[..., half_size:]
    cos_val = jnp.cos(angles)[:, None, :]
    sin_val = jnp.sin(angles)[:, None, :]
    turned = jnp.concatenate(
        [front_half * cos_val - back_half * sin_val, front_half * sin_val + back_half * cos_val],
        axis=-1,
    )
    if scale is not None:
        turned = turned * jnp.float32(scale)
    return turned


def scene_of(positions, scene_end):
    return jnp.sum((positions[:, None] >= scene_end[None, :]).astype(jnp.int32), axis=1)


LANES = 128


def make_kernel(piece_rows, heads, nq, has_state, finalize, TK):
    n_pieces = len(piece_rows)

    def kernel(lo_ref, hi_ref, q_ref, qs_ref, *rest):
        piece_refs = rest[: 2 * n_pieces]
        rest = rest[2 * n_pieces :]
        if has_state:
            m_in, acc_in = rest[:2]
            rest = rest[2:]
        outs = rest
        i = pl.program_id(0)
        tq = q_ref.shape[1]
        pad = jnp.zeros((tq, LANES - HD), jnp.bfloat16)
        qx = [jnp.concatenate([q_ref[h], pad], axis=1) for h in range(heads)]
        qs = jnp.tile(qs_ref[...], (1, TK // LANES))
        v_lanes = lax.broadcasted_iota(jnp.int32, (TK, LANES), 1) >= HD
        if has_state:
            carry = tuple((m_in[h], acc_in[h]) for h in range(heads))
        else:
            carry = tuple(
                (
                    jnp.full((tq, LANES), neg_big, jnp.float32),
                    jnp.zeros((tq, LANES), jnp.float32),
                )
                for h in range(heads)
            )
        for p in range(n_pieces):
            kv_ref, ks_ref = piece_refs[2 * p : 2 * p + 2]
            base = p * nq + i

            def body(j, carry, kv_ref=kv_ref, ks_ref=ks_ref):
                start = pl.multiple_of(j * TK, TK)
                allowed = qs == ks_ref[:, pl.ds(start, TK)]
                new = []
                for h in range(heads):
                    m, acc = carry[h]
                    kvt = kv_ref[h, pl.ds(start, TK), :]
                    s = lax.dot_general(
                        qx[h], kvt, (((1,), (1,)), ((), ())), preferred_element_type=jnp.float32
                    )
                    s = jnp.where(allowed, s, neg_big)
                    m_new = jnp.maximum(m, jnp.max(s, axis=1)[:, None])
                    p_w = jnp.exp(s - jnp.tile(m_new, (1, TK // LANES)))
                    alpha = jnp.exp(m - m_new)
                    pb = p_w.astype(jnp.bfloat16)
                    rhs = jnp.where(v_lanes, kvt, jnp.ones_like(kvt))
                    acc = alpha * acc + jnp.dot(pb, rhs, preferred_element_type=jnp.float32)
                    new.append((m_new, acc))
                return tuple(new)

            carry = lax.fori_loop(lo_ref[base], hi_ref[base], body, carry)
        if finalize:
            for h in range(heads):
                m, acc = carry[h]
                outs[0][h] = (acc[:, HD:] / acc[:, :HD]).astype(outs[0].dtype)
        else:
            for h in range(heads):
                m, acc = carry[h]
                outs[0][h] = m
                outs[1][h] = acc

    return kernel


def attend(q_h, q_scene, pieces, lo, hi, state, finalize, tk):
    heads, qlen, _ = q_h.shape
    nq = qlen // TQ
    piece_rows = [kv.shape[1] for kv, _ in pieces]
    has_state = state is not None
    kernel = make_kernel(piece_rows, heads, nq, has_state, finalize, tk)
    in_specs = [
        pl.BlockSpec((heads, TQ, HD), lambda i, *_: (0, i, 0)),
        pl.BlockSpec((TQ, LANES), lambda i, *_: (i, 0)),
    ]
    args = [q_h, q_scene]
    for kv, ks in pieces:
        rows = kv.shape[1]
        in_specs.append(pl.BlockSpec((heads, rows, LANES), lambda i, *_: (0, 0, 0)))
        in_specs.append(pl.BlockSpec((1, rows), lambda i, *_: (0, 0)))
        args += [kv, ks]
    state_specs = [pl.BlockSpec((heads, TQ, LANES), lambda i, *_: (0, i, 0)) for _ in range(2)]
    state_shapes = [jax.ShapeDtypeStruct((heads, qlen, LANES), jnp.float32) for _ in range(2)]
    if has_state:
        in_specs += state_specs
        args += list(state)
    if finalize:
        out_specs = [pl.BlockSpec((heads, TQ, HD), lambda i, *_: (0, i, 0))]
        out_shape = [jax.ShapeDtypeStruct((heads, qlen, HD), jnp.bfloat16)]
    else:
        out_specs = state_specs
        out_shape = state_shapes
    return pl.pallas_call(
        kernel,
        out_shape=out_shape,
        grid_spec=pltpu.PrefetchScalarGridSpec(
            num_scalar_prefetch=2,
            grid=(nq,),
            in_specs=in_specs,
            out_specs=out_specs,
        ),
        compiler_params=pltpu.CompilerParams(dimension_semantics=("arbitrary",)),
    )(lo, hi, *args)


def local(queries, keys, values, coords, lengths):
    tok_dev, all_cols = queries.shape
    head_count = lax.axis_size("head")
    seq_count = lax.axis_size("seq")
    head_cols = all_cols // head_count
    local_heads = head_cols // HD
    group_len = tok_dev * head_count
    total_len = group_len * seq_count
    near = min(MOST, group_len)
    far = MOST - near

    def head_major(x):
        width = x.shape[-1]
        return x.reshape(tok_dev, head_count, local_heads, width).transpose(1, 2, 0, 3)

    angles = rotary_angles(coords)
    q_rot = head_major(rotate_rows(queries, angles, score_scale).astype(jnp.bfloat16))
    k_rot = rotate_rows(keys, angles).astype(jnp.bfloat16)
    v_rows = values.reshape(tok_dev, -1, HD)
    kv_src = head_major(jnp.concatenate([k_rot, v_rows], axis=-1))
    kv = lax.all_to_all(kv_src, "head", split_axis=0, concat_axis=2, tiled=True)
    kv = kv.reshape(local_heads, group_len, 2 * HD)
    q_h = lax.all_to_all(q_rot, "head", split_axis=0, concat_axis=2, tiled=True)
    q_h = q_h.reshape(local_heads, group_len, HD)

    half = group_len - far
    below_hi = shifted(kv[:, half:], "seq", 1)
    below_lo = shifted(kv[:, :half], "seq", 1)
    above_lo = shifted(kv[:, :far], "seq", -1)
    above_hi = shifted(kv[:, far:], "seq", -1)
    near_pieces = [
        (below_lo, -group_len),
        (below_hi, -far),
        (above_lo, group_len),
        (above_hi, group_len + far),
    ]
    far_pieces = []
    if far > 0:
        below2 = shifted(below_hi, "seq", 1)
        above2 = shifted(above_lo, "seq", -1)
        far_pieces = [(below2, -group_len - far), (above2, 2 * group_len)]

    own_start = lax.axis_index("seq") * group_len
    scene_end = jnp.cumsum(lengths).astype(jnp.int32)
    scene_begin = scene_end - lengths
    q_pos = own_start + jnp.arange(group_len, dtype=jnp.int32)
    q_scene = scene_of(q_pos, scene_end)
    first_scene = q_scene[::TQ]
    last_scene = q_scene[TQ - 1 :: TQ]
    span_lo = jnp.take(scene_begin, first_scene)
    span_hi = jnp.take(scene_end, last_scene)

    def tables(piece_list, TK):
        los, his, prepared = [], [], []
        for kvp, offset in piece_list:
            rows = kvp.shape[1]
            p0 = own_start + offset
            k_pos = p0 + jnp.arange(rows, dtype=jnp.int32)
            k_valid = (k_pos >= 0) & (k_pos < total_len)
            k_scene = jnp.where(k_valid, scene_of(k_pos, scene_end), -1).astype(jnp.int32)
            lo = jnp.clip(span_lo - p0, 0, rows)
            hi = jnp.clip(span_hi - p0, 0, rows)
            klo = lo // TK
            khi = jnp.maximum((hi + TK - 1) // TK, klo)
            los.append(klo)
            his.append(khi)
            prepared.append((kvp, k_scene.reshape(1, rows)))
        return (
            jnp.concatenate(los).astype(jnp.int32),
            jnp.concatenate(his).astype(jnp.int32),
            prepared,
        )

    q_scene_col = jnp.broadcast_to(q_scene.astype(jnp.int32)[:, None], (group_len, LANES))
    if far_pieces:
        first = [(kv, 0), (below_hi, -far), (above_lo, group_len)]
        second = [(below_lo, -group_len), (above_hi, group_len + far)] + far_pieces
    else:
        first = [(kv, 0)]
        second = near_pieces
    lo0, hi0, prep0 = tables(first, TK)
    state = attend(q_h, q_scene_col, prep0, lo0, hi0, None, False, TK)
    lo1, hi1, prep1 = tables(second, TK_HALO)
    out_h = attend(q_h, q_scene_col, prep1, lo1, hi1, state, True, TK_HALO)[0]

    out_src = out_h.reshape(local_heads, head_count, tok_dev, HD)
    back = lax.all_to_all(out_src, "head", split_axis=1, concat_axis=0, tiled=True)
    back = back.reshape(head_count * local_heads, tok_dev, HD)
    return back.transpose(1, 0, 2).reshape(tok_dev, all_cols)


def solution(mesh):
    in_specs = (
        P(("dp", "seq", "head"), None),
        P(("dp", "seq", "head"), None),
        P(("dp", "seq", "head"), None),
        P(None, ("dp", "seq", "head")),
        P("dp"),
    )
    out_specs = P(("dp", "seq", "head"), None)
    return jax.shard_map(local, mesh=mesh, in_specs=in_specs, out_specs=out_specs, check_vma=False)
```

```python
import jax
import jax.numpy as jnp
from jax import lax
from jax.experimental import pallas as pl
from jax.experimental.pallas import tpu as pltpu
from jax.sharding import PartitionSpec as P

HD = 64
MOST = 1536

score_scale = 0.125
neg_big = -1e30

TQ = 256
TK = 512
TK_HALO = 256


def shifted(block, axis, distance):
    devices = range(lax.axis_size(axis))
    route = [(i - distance, i) for i in devices if i - distance in devices]
    return lax.ppermute(block, axis, route)


def rotary_angles(coords):
    pair_count = HD // 2
    pair_id = jnp.arange(pair_count, dtype=jnp.int32)
    axis_of = 3 * pair_id // pair_count
    exponent = (3 * pair_id % pair_count).astype(jnp.float32) / pair_count
    frequency = jnp.power(jnp.float32(100.0), -exponent)
    position = coords.astype(jnp.float32)
    angles = jnp.zeros((coords.shape[1], pair_count), jnp.float32)
    for axis_id in range(3):
        picked = jnp.where(axis_of == axis_id, frequency, jnp.float32(0.0))
        angles = angles + position[axis_id][:, None] * picked[None, :]
    return angles


def rotate_rows(source, angles, scale=None):
    row_count = source.shape[0]
    per_head = source.reshape(row_count, -1, HD).astype(jnp.float32)
    half_size = HD // 2
    front_half = per_head[..., :half_size]
    back_half = per_head[..., half_size:]
    cos_val = jnp.cos(angles)[:, None, :]
    sin_val = jnp.sin(angles)[:, None, :]
    turned = jnp.concatenate(
        [front_half * cos_val - back_half * sin_val, front_half * sin_val + back_half * cos_val],
        axis=-1,
    )
    if scale is not None:
        turned = turned * jnp.float32(scale)
    return turned


def scene_of(positions, scene_end):
    return jnp.sum((positions[:, None] >= scene_end[None, :]).astype(jnp.int32), axis=1)


LANES = 128


def make_kernel(piece_rows, heads, nq, has_state, finalize, TK):
    n_pieces = len(piece_rows)

    def kernel(lo_ref, hi_ref, q_ref, qs_ref, *rest):
        piece_refs = rest[: 2 * n_pieces]
        rest = rest[2 * n_pieces :]
        if has_state:
            m_in, acc_in = rest[:2]
            rest = rest[2:]
        outs = rest
        i = pl.program_id(0)
        tq = q_ref.shape[1]
        pad = jnp.zeros((tq, LANES - HD), jnp.bfloat16)
        qx = [jnp.concatenate([q_ref[h], pad], axis=1) for h in range(heads)]
        qs = jnp.broadcast_to(qs_ref[...], (tq, TK))
        v_lanes = lax.broadcasted_iota(jnp.int32, (TK, LANES), 1) >= HD
        if has_state:
            carry = tuple((m_in[h], acc_in[h]) for h in range(heads))
        else:
            carry = tuple(
                (
                    jnp.full((tq, LANES), neg_big, jnp.float32),
                    jnp.zeros((tq, LANES), jnp.float32),
                )
                for h in range(heads)
            )
        for p in range(n_pieces):
            kv_ref, ks_ref = piece_refs[2 * p : 2 * p + 2]
            base = p * nq + i

            def body(j, carry, kv_ref=kv_ref, ks_ref=ks_ref):
                start = pl.multiple_of(j * TK, TK)
                allowed = qs == ks_ref[:, pl.ds(start, TK)]
                new = []
                for h in range(heads):
                    m, acc = carry[h]
                    kvt = kv_ref[h, pl.ds(start, TK), :]
                    s = lax.dot_general(
                        qx[h], kvt, (((1,), (1,)), ((), ())), preferred_element_type=jnp.float32
                    )
                    s = jnp.where(allowed, s, neg_big)
                    m_new = jnp.maximum(m, jnp.max(s, axis=1)[:, None])
                    p_w = jnp.exp(s - jnp.tile(m_new, (1, TK // LANES)))
                    alpha = jnp.exp(m - m_new)
                    pb = p_w.astype(jnp.bfloat16)
                    rhs = jnp.where(v_lanes, kvt, jnp.ones_like(kvt))
                    acc = alpha * acc + jnp.dot(pb, rhs, preferred_element_type=jnp.float32)
                    new.append((m_new, acc))
                return tuple(new)

            carry = lax.fori_loop(lo_ref[base], hi_ref[base], body, carry)
        if finalize:
            for h in range(heads):
                m, acc = carry[h]
                outs[0][h] = (acc[:, HD:] / acc[:, :HD]).astype(outs[0].dtype)
        else:
            for h in range(heads):
                m, acc = carry[h]
                outs[0][h] = m
                outs[1][h] = acc

    return kernel


def attend(q_h, q_scene, pieces, lo, hi, state, finalize, tk):
    heads, qlen, _ = q_h.shape
    nq = qlen // TQ
    piece_rows = [kv.shape[1] for kv, _ in pieces]
    has_state = state is not None
    kernel = make_kernel(piece_rows, heads, nq, has_state, finalize, tk)
    in_specs = [
        pl.BlockSpec((heads, TQ, HD), lambda i, *_: (0, i, 0)),
        pl.BlockSpec((TQ, 1), lambda i, *_: (i, 0)),
    ]
    args = [q_h, q_scene]
    for kv, ks in pieces:
        rows = kv.shape[1]
        in_specs.append(pl.BlockSpec((heads, rows, LANES), lambda i, *_: (0, 0, 0)))
        in_specs.append(pl.BlockSpec((1, rows), lambda i, *_: (0, 0)))
        args += [kv, ks]
    state_specs = [pl.BlockSpec((heads, TQ, LANES), lambda i, *_: (0, i, 0)) for _ in range(2)]
    state_shapes = [jax.ShapeDtypeStruct((heads, qlen, LANES), jnp.float32) for _ in range(2)]
    if has_state:
        in_specs += state_specs
        args += list(state)
    if finalize:
        out_specs = [pl.BlockSpec((heads, TQ, HD), lambda i, *_: (0, i, 0))]
        out_shape = [jax.ShapeDtypeStruct((heads, qlen, HD), jnp.bfloat16)]
    else:
        out_specs = state_specs
        out_shape = state_shapes
    return pl.pallas_call(
        kernel,
        out_shape=out_shape,
        grid_spec=pltpu.PrefetchScalarGridSpec(
            num_scalar_prefetch=2,
            grid=(nq,),
            in_specs=in_specs,
            out_specs=out_specs,
        ),
        compiler_params=pltpu.CompilerParams(dimension_semantics=("arbitrary",)),
    )(lo, hi, *args)


def local(queries, keys, values, coords, lengths):
    tok_dev, all_cols = queries.shape
    head_count = lax.axis_size("head")
    seq_count = lax.axis_size("seq")
    head_cols = all_cols // head_count
    local_heads = head_cols // HD
    group_len = tok_dev * head_count
    total_len = group_len * seq_count
    near = min(MOST, group_len)
    far = MOST - near

    def head_major(x):
        width = x.shape[-1]
        return x.reshape(tok_dev, head_count, local_heads, width).transpose(1, 2, 0, 3)

    angles = rotary_angles(coords)
    q_rot = head_major(rotate_rows(queries, angles, score_scale).astype(jnp.bfloat16))
    k_rot = rotate_rows(keys, angles).astype(jnp.bfloat16)
    v_rows = values.reshape(tok_dev, -1, HD)
    kv_src = head_major(jnp.concatenate([k_rot, v_rows], axis=-1))
    kv = lax.all_to_all(kv_src, "head", split_axis=0, concat_axis=2, tiled=True)
    kv = kv.reshape(local_heads, group_len, 2 * HD)
    q_h = lax.all_to_all(q_rot, "head", split_axis=0, concat_axis=2, tiled=True)
    q_h = q_h.reshape(local_heads, group_len, HD)

    half = group_len - far
    below_hi = shifted(kv[:, half:], "seq", 1)
    below_lo = shifted(kv[:, :half], "seq", 1)
    above_lo = shifted(kv[:, :far], "seq", -1)
    above_hi = shifted(kv[:, far:], "seq", -1)
    near_pieces = [
        (below_lo, -group_len),
        (below_hi, -far),
        (above_lo, group_len),
        (above_hi, group_len + far),
    ]
    far_pieces = []
    if far > 0:
        below2 = shifted(below_hi, "seq", 1)
        above2 = shifted(above_lo, "seq", -1)
        far_pieces = [(below2, -group_len - far), (above2, 2 * group_len)]

    own_start = lax.axis_index("seq") * group_len
    scene_end = jnp.cumsum(lengths).astype(jnp.int32)
    scene_begin = scene_end - lengths
    q_pos = own_start + jnp.arange(group_len, dtype=jnp.int32)
    q_scene = scene_of(q_pos, scene_end)
    first_scene = q_scene[::TQ]
    last_scene = q_scene[TQ - 1 :: TQ]
    span_lo = jnp.take(scene_begin, first_scene)
    span_hi = jnp.take(scene_end, last_scene)

    def tables(piece_list, TK):
        los, his, prepared = [], [], []
        for kvp, offset in piece_list:
            rows = kvp.shape[1]
            p0 = own_start + offset
            k_pos = p0 + jnp.arange(rows, dtype=jnp.int32)
            k_valid = (k_pos >= 0) & (k_pos < total_len)
            k_scene = jnp.where(k_valid, scene_of(k_pos, scene_end), -1).astype(jnp.int32)
            lo = jnp.clip(span_lo - p0, 0, rows)
            hi = jnp.clip(span_hi - p0, 0, rows)
            klo = lo // TK
            khi = jnp.maximum((hi + TK - 1) // TK, klo)
            los.append(klo)
            his.append(khi)
            prepared.append((kvp, k_scene.reshape(1, rows)))
        return (
            jnp.concatenate(los).astype(jnp.int32),
            jnp.concatenate(his).astype(jnp.int32),
            prepared,
        )

    q_scene_col = q_scene.astype(jnp.int32).reshape(group_len, 1)
    if far_pieces:
        first = [(kv, 0), (below_hi, -far), (above_lo, group_len)]
        second = [(below_lo, -group_len), (above_hi, group_len + far)] + far_pieces
    else:
        first = [(kv, 0)]
        second = near_pieces
    lo0, hi0, prep0 = tables(first, TK)
    state = attend(q_h, q_scene_col, prep0, lo0, hi0, None, False, TK)
    lo1, hi1, prep1 = tables(second, TK_HALO)
    out_h = attend(q_h, q_scene_col, prep1, lo1, hi1, state, True, TK_HALO)[0]

    out_src = out_h.reshape(local_heads, head_count, tok_dev, HD)
    back = lax.all_to_all(out_src, "head", split_axis=1, concat_axis=0, tiled=True)
    back = back.reshape(head_count * local_heads, tok_dev, HD)
    return back.transpose(1, 0, 2).reshape(tok_dev, all_cols)


def solution(mesh):
    in_specs = (
        P(("dp", "seq", "head"), None),
        P(("dp", "seq", "head"), None),
        P(("dp", "seq", "head"), None),
        P(None, ("dp", "seq", "head")),
        P("dp"),
    )
    out_specs = P(("dp", "seq", "head"), None)
    return jax.shard_map(local, mesh=mesh, in_specs=in_specs, out_specs=out_specs, check_vma=False)
```
